512 devices in a mesh: seq: 128 (over y, z, core), kvh: 4 (over x).
Axes of the slice: x: 4, y: 8, z: 8, core: 2. Of those that a mesh axis runs over, the one named last changes fastest.
Arguments:
- queries: bfloat16 [8192, 64, 128], P('seq', 'kvh'), may hold values from -15 to 15
- stretch_kv: bfloat16 [2, 8192, 8, 128], P(None, 'seq', 'kvh'), may hold values from -15 to 15
- cache_kv: bfloat16 [2, 128, 2048, 8, 128], P(None, 'seq', None, 'kvh'), may hold values from -15 to 15
- selection: int32 [8, 8192, 3], P('kvh', 'seq'), may hold values from 0 to 127, all different within a row; in each aligned block of 64 rows (0 to 63, 64 to 127, ..., all dimensions but the last counted through in order) at most 2 rows name the same one
- block_owner: int32 [128], replicated, may hold values from 0 to 127, each once
Outputs:
- attended: bfloat16 [8192, 8192], P(('seq', 'kvh'))
The draws below stay inside these ranges and needn't reach their ends.
Inputs may be any that keep to these rules, and one draw needn't show every extreme that they name: `selection`: each KV head and token names 3 different blocks. Among the 64 tokens of one index of seq, for one KV head, no block is named more than 2 times, and some block is named exactly 2 times. `block_owner`: A permutation: each storage position holds exactly one block.
All inputs are finite; a program needn't handle non-finite values.
Results may differ from the reference program's by a relative error of at most 0.0051.
Values may be sent and summed in bfloat16 or wider, within the bound.
No kernel may reach another device: no remote copies, remote signals or barrier semaphores. Data moves between devices by JAX's collectives and lax.ppermute only.
A program may use at most 128 MiB of HBM per device.

```python
import math
import jax
import jax.numpy as jnp
import numpy as np
from jax import lax

QUERY_HEAD_COUNT = 64
KEY_VALUE_HEADS = 8
HEAD_SIZE = 128
TOKENS_PER_SEQ = 64
BLOCK_TOKENS = 2048
PICKED_BLOCKS = 3
STRETCH_TOKENS = 8192
CACHED_BLOCKS = 128
BLOCK_PICK_LIMIT = 2
CUR = 32
N_SEQ = 128


def coarse_field(key, shape):
    return jax.random.normal(jax.random.fold_in(key, 13), shape, jnp.float32)


def draw_queries(key, part):
    score_field = 2.0 * coarse_field(jax.random.fold_in(key, 1), (STRETCH_TOKENS, QUERY_HEAD_COUNT, HEAD_SIZE))
    return jnp.clip(score_field, -15.0, 15.0).astype(jnp.bfloat16)


def draw_stretch_kv(key, part):
    score_field = coarse_field(jax.random.fold_in(key, 2), (2, STRETCH_TOKENS, KEY_VALUE_HEADS, HEAD_SIZE))
    return jnp.clip(score_field, -15.0, 15.0).astype(jnp.bfloat16)


def draw_cache_kv(key, part):
    score_field = coarse_field(jax.random.fold_in(key, 3), (2, CACHED_BLOCKS, BLOCK_TOKENS, KEY_VALUE_HEADS, HEAD_SIZE))
    return jnp.clip(score_field, -15.0, 15.0).astype(jnp.bfloat16)


def routed_block(key, own, number, rows, number_of, top, limit, slope):
    sequence = jax.random.permutation(key, number_of)
    packed, common = shares(number_of, rows * top, limit, slope, True), shares(number_of, rows * top, limit, slope, False)
    places = jnp.arange(number_of)

    def named(tallies, offset_by):
        used = int((tallies > 0).sum())
        fixed = max(1, used // 4)
        shifted = fixed + (places - fixed + offset_by * (used - fixed)) % max(1, number_of - fixed)
        return jnp.zeros((number_of,), jnp.int32).at[sequence[jnp.where(places < fixed, places, shifted)]].set(jnp.asarray(tallies, jnp.int32))

    tallies = jnp.where(number % 4 == 0, named(packed, number // 4), named(common, number - number // 4 - 1))
    mixed = jax.random.permutation(jax.random.fold_in(own, 3), number_of)
    giver, receiver = mixed[0:number_of // 2 * 2:2], mixed[1:number_of // 2 * 2:2]
    room = jnp.minimum(tallies[giver] - 1, limit - tallies[receiver]) // 2
    room = jnp.where((giver == sequence[0]) | (receiver == sequence[0]) | (tallies[receiver] == 0), 0, jnp.maximum(room, 0))
    shifted = jax.random.randint(jax.random.fold_in(own, 4), (number_of // 2,), 0, 1 << 20) % (room + 1)
    tallies = tallies.at[giver].add(-shifted).at[receiver].add(shifted)
    members = jnp.searchsorted(jnp.cumsum(tallies), jnp.arange(rows * top), side="right").astype(jnp.int32)
    listing = members.reshape(top, rows).T
    listing = listing[jax.random.permutation(jax.random.fold_in(own, 1), rows)]
    offset_by = jax.random.randint(jax.random.fold_in(own, 2), (rows, 1), 0, top)
    return jnp.take_along_axis(listing, (jnp.arange(top)[None, :] + offset_by) % top, axis=1)


def shares(amount, total, most, skew, full):
    weights = [(1 << 20) // math.isqrt(rank ** skew) + 1 for rank in range(1, amount + 1)]
    largest = most if full else min(most, max(-(-total // amount), total * weights[0] // sum(weights)))
    least = 1 if total - largest >= amount - 1 else 0
    given, spare = [largest] + [least] * (amount - 1), total - largest - least * (amount - 1)
    while spare > 0:
        candidates = [i for i in range(1, amount) if given[i] < largest] or [i for i in range(1, amount) if given[i] < most]
        mass, remaining = sum([weights[i] for i in candidates]), spare
        for i in candidates:
            more = min(most - given[i], max(1, remaining * weights[i] // mass), spare)
            given[i] = given[i] + more
            spare = spare - more
    return np.array(given)


def setup_inputs(seed: int = 0) -> dict:
    splits = jax.random.split(jax.random.key(seed), 6)
    queries = draw_queries(jax.random.fold_in(splits[5], 71), 0)
    stretch_kv = draw_stretch_kv(jax.random.fold_in(splits[5], 71), 0)
    cache_kv = draw_cache_kv(jax.random.fold_in(splits[5], 71), 0)
    selection_keys = jax.random.split(jax.random.fold_in(splits[3], 1), KEY_VALUE_HEADS * STRETCH_TOKENS // TOKENS_PER_SEQ)
    selection_turns = jax.random.permutation(jax.random.fold_in(splits[3], 3), KEY_VALUE_HEADS * STRETCH_TOKENS // TOKENS_PER_SEQ)
    selection = jax.vmap(lambda own, number: routed_block(jax.random.fold_in(splits[3], 2), own, number, TOKENS_PER_SEQ, CACHED_BLOCKS, PICKED_BLOCKS, BLOCK_PICK_LIMIT, 2))(selection_keys, selection_turns).reshape((KEY_VALUE_HEADS, STRETCH_TOKENS, PICKED_BLOCKS))
    block_owner = jax.random.permutation(splits[4], CACHED_BLOCKS).astype(jnp.int32)
    return dict(queries=queries, stretch_kv=stretch_kv, cache_kv=cache_kv, selection=selection, block_owner=block_owner)


def reference(queries, stretch_kv, cache_kv, selection, block_owner):
    tokens_all, query_heads, head_dim = queries.shape
    kv_heads = stretch_kv.shape[2]
    group_size = query_heads // kv_heads
    scaling = 1.0 / math.sqrt(head_dim)
    piece_rows = TOKENS_PER_SEQ
    window_rows = CUR * piece_rows
    piece_count = tokens_all // piece_rows
    grouped = queries.reshape(tokens_all, kv_heads, group_size, head_dim)
    by_head = jnp.transpose(grouped, (1, 0, 2, 3))
    stretch_by_head = jnp.transpose(stretch_kv, (0, 2, 1, 3))
    padded_kv = jnp.pad(stretch_by_head, ((0, 0), (0, 0), ((CUR - 1) * piece_rows, 0), (0, 0)))
    anchor = jnp.int32(0)

    def current(index):
        kv_index = index // piece_count
        start = index % piece_count * piece_rows
        query_rows = lax.dynamic_slice(by_head, (kv_index, start, anchor, anchor), (1, piece_rows, group_size, head_dim))[0].astype(jnp.float32)
        stacked = lax.dynamic_slice(padded_kv, (anchor, kv_index, start, anchor), (2, 1, window_rows, head_dim))[:, 0].astype(jnp.float32)
        key_place = start - (CUR - 1) * piece_rows + jnp.arange(window_rows, dtype=jnp.int32)
        query_place = start + jnp.arange(piece_rows, dtype=jnp.int32)
        allowed = (key_place[None, :] >= 0) & (key_place[None, :] <= query_place[:, None])
        scores = jnp.einsum('tgd,kd->tgk', query_rows, stacked[0]) * scaling
        scores = jnp.where(allowed[:, None, :], scores, -jnp.inf)
        highest = lax.optimization_barrier(jnp.max(scores, axis=2))
        raw_weights = jnp.exp(scores - highest[..., None])
        weight_sum = lax.optimization_barrier(jnp.sum(raw_weights, axis=2))
        rounded = lax.optimization_barrier(raw_weights.astype(jnp.bfloat16)).astype(jnp.float32)
        blended = jnp.einsum('tgk,kd->tgd', rounded, stacked[1]) / weight_sum[..., None]
        return (blended, highest + jnp.log(weight_sum))
    cur_out, cur_lse = lax.map(current, jnp.arange(kv_heads * piece_count, dtype=jnp.int32))
    cur_out = jnp.transpose(cur_out.reshape(kv_heads, tokens_all, group_size, head_dim), (1, 0, 2, 3))
    cur_lse = jnp.transpose(cur_lse.reshape(kv_heads, tokens_all, group_size), (1, 0, 2))
    capacity = BLOCK_PICK_LIMIT * N_SEQ
    head_rows = jnp.arange(kv_heads, dtype=jnp.int32)[:, None]

    def visit(carry, block_id):
        running, log_total = carry
        holder = block_owner[block_id]
        stored = lax.dynamic_index_in_dim(cache_kv, holder, 1, keepdims=False).astype(jnp.float32)
        chosen = jnp.any(selection == block_id, axis=2)
        order = jnp.argsort(jnp.where(chosen, 0, 1), axis=1, stable=True)[:, :capacity].astype(jnp.int32)
        usable = jnp.take_along_axis(chosen, order, axis=1)
        query_rows = grouped[order, head_rows].astype(jnp.float32)
        scores = jnp.einsum('hcgd,khd->hcgk', query_rows, stored[0]) * scaling
        highest = lax.optimization_barrier(jnp.max(scores, axis=3))
        raw_weights = jnp.exp(scores - highest[..., None])
        weight_sum = lax.optimization_barrier(jnp.sum(raw_weights, axis=3))
        rounded = lax.optimization_barrier(raw_weights.astype(jnp.bfloat16)).astype(jnp.float32)
        blended = (jnp.einsum('hcgk,khd->hcgd', rounded, stored[1]) / weight_sum[..., None]).astype(jnp.bfloat16)
        block_lse = highest + jnp.log(weight_sum)
        old_lse = log_total[order, head_rows]
        old_mix = running[order, head_rows]
        new_lse = jnp.logaddexp(old_lse, block_lse)
        new_mix = old_mix * jnp.exp(old_lse - new_lse)[..., None] + blended.astype(jnp.float32) * jnp.exp(block_lse - new_lse)[..., None]
        keeping = usable[..., None]
        running = running.at[order, head_rows].set(jnp.where(keeping[..., None], new_mix, old_mix))
        log_total = log_total.at[order, head_rows].set(jnp.where(keeping, new_lse, old_lse))
        return ((running, log_total), None)
    (running, log_total), _ = lax.scan(visit, (cur_out, cur_lse), jnp.arange(CACHED_BLOCKS, dtype=jnp.int32))
    return running.astype(jnp.bfloat16).reshape(tokens_all, query_heads * head_dim)
```

```python
import math

import jax
import jax.numpy as jnp
from jax import lax
from jax.sharding import PartitionSpec as P

BLOCK_TOKENS = 2048
BLOCK_PICK_LIMIT = 2
WINDOW_SHIFTS = (8, 4, 16, 2, 1)


def shifted(value, axis, steps):
    count = lax.axis_size(axis)
    initial, last = (max(0, -steps), min(count, count - steps))
    return lax.ppermute(value, axis, [(source, source + steps) for source in range(initial, last)])


def gather_window(stretch_kv, span_devices):
    stack = stretch_kv[None]
    offsets = [0]
    for step in WINDOW_SHIFTS:
        if len(offsets) >= span_devices:
            break
        arrived = shifted(stack, "seq", step)
        stack = jnp.concatenate([stack, arrived], axis=0)
        offsets = offsets + [o + step for o in offsets]
    return stack, offsets


def window_attention(grouped, window, offsets, seq_place, scaling):
    rows_local, kv_heads, group_size, head_dim = grouped.shape
    blocks = window.shape[0]
    keys = jnp.transpose(window[:, 0], (2, 0, 1, 3)).reshape(kv_heads, blocks * rows_local, head_dim)
    values = jnp.transpose(window[:, 1], (2, 0, 1, 3)).reshape(kv_heads, blocks * rows_local, head_dim)
    offset_arr = jnp.asarray(offsets, jnp.int32)
    exists = (seq_place - offset_arr) >= 0
    key_pos = jnp.arange(rows_local, dtype=jnp.int32)
    query_pos = jnp.arange(rows_local, dtype=jnp.int32)
    causal = (offset_arr[None, :, None] > 0) | (key_pos[None, None, :] <= query_pos[:, None, None])
    allowed = (exists[None, :, None] & causal).reshape(rows_local, blocks * rows_local)
    scores = (
        jnp.einsum("thgd,hkd->htgk", grouped, keys, preferred_element_type=jnp.float32) * scaling
    )
    scores = jnp.where(allowed[None, :, None, :], scores, -jnp.inf)
    highest = jnp.max(scores, axis=3)
    raw_weights = jnp.exp(scores - highest[..., None])
    weight_sum = jnp.sum(raw_weights, axis=3)
    blended = jnp.einsum(
        "htgk,hkd->htgd",
        raw_weights.astype(jnp.bfloat16),
        values,
        preferred_element_type=jnp.float32,
    ) / weight_sum[..., None]
    return blended, highest + jnp.log(weight_sum)


def serve_blocks(arrived, cache_kv, scaling):
    sources, items, kv_heads, group_size, head_dim = arrived.shape
    outputs = []
    log_sums = []
    for kv_index in range(kv_heads):
        query_rows = arrived[:, :, kv_index].reshape(sources * items * group_size, head_dim)
        key_rows = cache_kv[0, 0, :, kv_index]
        value_rows = cache_kv[1, 0, :, kv_index]
        scores = (
            jnp.einsum("rd,kd->rk", query_rows, key_rows, preferred_element_type=jnp.float32)
            * scaling
        )
        highest = jnp.max(scores, axis=1, keepdims=True)
        raw_weights = jnp.exp(scores - highest)
        weight_sum = jnp.sum(raw_weights, axis=1, keepdims=True)
        blended = (
            jnp.einsum(
                "rk,kd->rd",
                raw_weights.astype(jnp.bfloat16),
                value_rows,
                preferred_element_type=jnp.float32,
            )
            / weight_sum
        )
        outputs.append(blended.astype(jnp.bfloat16).reshape(sources, items, group_size, head_dim))
        log_sums.append((highest + jnp.log(weight_sum)).reshape(sources, items, group_size))
    partial_out = jnp.stack(outputs, axis=2)
    partial_lse = jnp.stack(log_sums, axis=2)
    returned = lax.all_to_all(partial_out, "seq", split_axis=0, concat_axis=0, tiled=True)
    returned_lse = lax.all_to_all(partial_lse, "seq", split_axis=0, concat_axis=0, tiled=True)
    return (returned, returned_lse)


def per_device(queries, stretch_kv, cache_kv, selection, block_owner):
    rows_local, query_heads, head_dim = queries.shape
    kv_heads = stretch_kv.shape[2]
    group_size = query_heads // kv_heads
    top_count = selection.shape[2]
    scaling = 1.0 / math.sqrt(head_dim)
    seq_count = lax.axis_size("seq")
    capacity = BLOCK_PICK_LIMIT
    span_devices = min(BLOCK_TOKENS // rows_local, seq_count)
    seq_place = lax.axis_index("seq")
    grouped = queries.reshape(rows_local, kv_heads, group_size, head_dim)
    requests = rows_local * top_count
    targets = block_owner[selection].reshape(kv_heads, requests)
    matches = (targets[:, :, None] == jnp.arange(seq_count, dtype=jnp.int32)[None, None, :]).astype(
        jnp.int32
    )
    places = jnp.sum((jnp.cumsum(matches, axis=1) - 1) * matches, axis=2)
    slots = targets * capacity + places
    one_hot = (
        slots[:, None, :] == jnp.arange(seq_count * capacity, dtype=jnp.int32)[None, :, None]
    ).astype(jnp.bfloat16)
    requested = jnp.repeat(jnp.swapaxes(grouped, 0, 1), top_count, axis=1).reshape(
        kv_heads, requests, group_size * head_dim
    )
    outgoing = jnp.einsum(
        "hsr,hrx->shx", one_hot, requested, preferred_element_type=jnp.float32
    ).astype(jnp.bfloat16)
    outgoing = outgoing.reshape(seq_count, capacity, kv_heads, group_size, head_dim)
    answers, answer_lse = serve_blocks(
        lax.all_to_all(outgoing, "seq", split_axis=0, concat_axis=0, tiled=True), cache_kv, scaling
    )
    window, offsets = gather_window(stretch_kv, span_devices)
    own_out, own_lse = window_attention(grouped, window, offsets, seq_place, scaling)
    head_rows = jnp.arange(kv_heads, dtype=jnp.int32)[:, None]
    picked = (
        jnp.einsum(
            "hsr,shx->hrx",
            one_hot,
            answers.reshape(seq_count * capacity, kv_heads, group_size * head_dim),
            preferred_element_type=jnp.float32,
        )
        .reshape(kv_heads, rows_local, top_count, group_size, head_dim)
    )
    picked_lse = answer_lse[targets, places, head_rows].reshape(
        kv_heads, rows_local, top_count, group_size
    )
    ceiling = jnp.maximum(own_lse, jnp.max(picked_lse, axis=2))
    own_weight = jnp.exp(own_lse - ceiling)
    far_weight = jnp.exp(picked_lse - ceiling[:, :, None])
    denominator = own_weight + jnp.sum(far_weight, axis=2)
    combined = (
        own_weight[..., None] * own_out + jnp.sum(far_weight[..., None] * picked, axis=2)
    ) / denominator[..., None]
    heads_out = (
        jnp.transpose(combined, (1, 0, 2, 3))
        .astype(jnp.bfloat16)
        .reshape(rows_local, query_heads * head_dim)
    )
    return lax.all_to_all(heads_out, "kvh", split_axis=0, concat_axis=1, tiled=True)


def solution(mesh):
    placed = (
        P("seq", "kvh", None),
        P(None, "seq", "kvh", None),
        P(None, "seq", None, "kvh", None),
        P("kvh", "seq", None),
        P(),
    )
    return jax.shard_map(
        per_device, mesh=mesh, in_specs=placed, out_specs=P(("seq", "kvh"), None), check_vma=False
    )
```

```python
import functools
import math

import jax
import jax.numpy as jnp
from jax import lax
from jax.experimental import pallas as pl
from jax.sharding import PartitionSpec as P

BLOCK_TOKENS = 2048
BLOCK_PICK_LIMIT = 2
WINDOW_SHIFTS = (8, 4, 16, 2, 1)


def shifted(value, axis, steps):
    count = lax.axis_size(axis)
    initial, last = (max(0, -steps), min(count, count - steps))
    return lax.ppermute(value, axis, [(source, source + steps) for source in range(initial, last)])


def gather_window(stretch_kv, span_devices):
    stack = stretch_kv[None]
    offsets = [0]
    for step in WINDOW_SHIFTS:
        if len(offsets) >= span_devices:
            break
        stack = jnp.concatenate([stack, shifted(stack, "seq", step)], axis=0)
        offsets = offsets + [o + step for o in offsets]
    return stack, offsets


def attend_kernel(masked, scaling, group_size, *refs):
    if masked:
        thr_ref, q_ref, k_ref, v_ref, o_ref, lse_ref = refs
    else:
        q_ref, k_ref, v_ref, o_ref, lse_ref = refs
    q = q_ref[...]
    q = q.reshape(-1, q.shape[-1])
    scores = (
        lax.dot_general(
            q, k_ref[...], (((1,), (1,)), ((), ())), preferred_element_type=jnp.float32
        )
        * scaling
    )
    if masked:
        token = lax.broadcasted_iota(jnp.int32, (scores.shape[0], 1), 0) // group_size
        scores = jnp.where(token >= thr_ref[...], scores, -jnp.inf)
    highest = jnp.max(scores, axis=1, keepdims=True)
    raw_weights = jnp.exp(scores - highest)
    weight_sum = jnp.sum(raw_weights, axis=1, keepdims=True)
    blended = (
        jnp.dot(raw_weights.astype(jnp.bfloat16), v_ref[...], preferred_element_type=jnp.float32)
        / weight_sum
    )
    o_ref[...] = blended.astype(o_ref.dtype).reshape(o_ref.shape)
    lse_ref[...] = highest + jnp.log(weight_sum)


def attend(q, q_block, q_map, heads, tiles, keys, values, out_dtype, scaling, group_size, thr=None):
    rows = q_block[0] * q_block[-2] if len(q_block) == 4 else q_block[-2]
    total_rows = rows * tiles
    key_count, head_dim = keys.shape[1], keys.shape[2]
    kv_spec = pl.BlockSpec((None, key_count, head_dim), lambda h, i: (h, 0, 0))
    in_specs = [pl.BlockSpec(q_block, q_map), kv_spec, kv_spec]
    operands = [q, keys, values]
    if thr is not None:
        in_specs = [pl.BlockSpec((1, key_count), lambda h, i: (0, 0))] + in_specs
        operands = [thr] + operands
    cost = pl.CostEstimate(
        flops=4 * heads * total_rows * key_count * head_dim,
        transcendentals=heads * total_rows * key_count,
        bytes_accessed=2 * (2 * heads * total_rows * head_dim + 2 * heads * key_count * head_dim),
    )
    return pl.pallas_call(
        functools.partial(attend_kernel, thr is not None, scaling, group_size),
        grid=(heads, tiles),
        in_specs=in_specs,
        out_specs=[
            pl.BlockSpec(q_block, q_map),
            pl.BlockSpec((None, rows, 1), lambda h, i: (h, i, 0)),
        ],
        out_shape=[
            jax.ShapeDtypeStruct(q.shape, out_dtype),
            jax.ShapeDtypeStruct((heads, total_rows, 1), jnp.float32),
        ],
        cost_estimate=cost,
    )(*operands)


def per_device(queries, stretch_kv, cache_kv, selection, block_owner):
    rows_local, query_heads, head_dim = queries.shape
    kv_heads = stretch_kv.shape[2]
    group_size = query_heads // kv_heads
    top_count = selection.shape[2]
    scaling = 1.0 / math.sqrt(head_dim)
    seq_count = lax.axis_size("seq")
    capacity = BLOCK_PICK_LIMIT
    span_devices = min(BLOCK_TOKENS // rows_local, seq_count)
    seq_place = lax.axis_index("seq")
    grouped = queries.reshape(rows_local, kv_heads, group_size, head_dim)
    requests = rows_local * top_count
    targets = block_owner[selection].reshape(kv_heads, requests)
    matches = (targets[:, :, None] == jnp.arange(seq_count, dtype=jnp.int32)[None, None, :]).astype(
        jnp.int32
    )
    places = jnp.sum((jnp.cumsum(matches, axis=1) - 1) * matches, axis=2)
    slots = targets * capacity + places
    one_hot = (
        (slots[:, None, :] == jnp.arange(seq_count * capacity, dtype=jnp.int32)[None, :, None])
        .astype(jnp.bfloat16)
        .reshape(kv_heads, seq_count, capacity, requests)
    )
    requested = jnp.repeat(jnp.swapaxes(grouped, 0, 1), top_count, axis=1).reshape(
        kv_heads, requests, group_size * head_dim
    )
    outgoing = jnp.einsum(
        "htcr,hrx->thcx", one_hot, requested, preferred_element_type=jnp.float32
    ).astype(jnp.bfloat16)
    slab = capacity * group_size
    outgoing = outgoing.reshape(seq_count, kv_heads, slab, head_dim)
    arrived = lax.all_to_all(outgoing, "seq", split_axis=0, concat_axis=0, tiled=True)
    cache_keys = jnp.swapaxes(cache_kv[0, 0], 0, 1)
    cache_values = jnp.swapaxes(cache_kv[1, 0], 0, 1)
    sources_per_tile = 32
    served, served_lse = attend(
        arrived,
        (sources_per_tile, None, slab, head_dim),
        lambda h, i: (i, h, 0, 0),
        kv_heads,
        seq_count // sources_per_tile,
        cache_keys,
        cache_values,
        jnp.bfloat16,
        scaling,
        group_size,
    )
    served_lse = jnp.swapaxes(served_lse.reshape(kv_heads, seq_count, slab), 0, 1)
    answers = lax.all_to_all(served, "seq", split_axis=0, concat_axis=0, tiled=True)
    answer_lse = lax.all_to_all(served_lse, "seq", split_axis=0, concat_axis=0, tiled=True)
    answers = answers.reshape(seq_count, kv_heads, capacity, group_size * head_dim)
    answer_lse = answer_lse.reshape(seq_count, kv_heads, capacity, group_size)
    window, offsets = gather_window(stretch_kv, span_devices)
    blocks = window.shape[0]
    window_keys = jnp.transpose(window[:, 0], (2, 0, 1, 3)).reshape(kv_heads, blocks * rows_local, head_dim)
    window_values = jnp.transpose(window[:, 1], (2, 0, 1, 3)).reshape(kv_heads, blocks * rows_local, head_dim)
    key_index = jnp.arange(blocks * rows_local, dtype=jnp.int32)
    key_offset = jnp.asarray(offsets, jnp.int32)[key_index // rows_local]
    threshold = jnp.where(
        seq_place - key_offset >= 0,
        jnp.where(key_offset == 0, key_index % rows_local, 0),
        rows_local,
    )[None, :]
    window_queries = jnp.swapaxes(grouped, 0, 1).reshape(kv_heads, rows_local * group_size, head_dim)
    own_out, own_lse = attend(
        window_queries,
        (None, rows_local * group_size, head_dim),
        lambda h, i: (h, 0, 0),
        kv_heads,
        1,
        window_keys,
        window_values,
        jnp.float32,
        scaling,
        group_size,
        threshold,
    )
    own_out = own_out.reshape(kv_heads, rows_local, group_size, head_dim)
    own_lse = own_lse.reshape(kv_heads, rows_local, group_size)
    head_rows = jnp.arange(kv_heads, dtype=jnp.int32)[:, None]
    picked = (
        jnp.einsum(
            "htcr,thcx->hrx",
            one_hot,
            answers,
            preferred_element_type=jnp.float32,
        )
        .reshape(kv_heads, rows_local, top_count, group_size, head_dim)
    )
    picked_lse = answer_lse[targets, head_rows, places].reshape(
        kv_heads, rows_local, top_count, group_size
    )
    ceiling = jnp.maximum(own_lse, jnp.max(picked_lse, axis=2))
    own_weight = jnp.exp(own_lse - ceiling)
    far_weight = jnp.exp(picked_lse - ceiling[:, :, None])
    denominator = own_weight + jnp.sum(far_weight, axis=2)
    combined = (
        own_weight[..., None] * own_out + jnp.sum(far_weight[..., None] * picked, axis=2)
    ) / denominator[..., None]
    heads_out = (
        jnp.transpose(combined, (1, 0, 2, 3))
        .astype(jnp.bfloat16)
        .reshape(rows_local, query_heads * head_dim)
    )
    return lax.all_to_all(heads_out, "kvh", split_axis=0, concat_axis=1, tiled=True)


def solution(mesh):
    placed = (
        P("seq", "kvh", None),
        P(None, "seq", "kvh", None),
        P(None, "seq", None, "kvh", None),
        P("kvh", "seq", None),
        P(),
    )
    return jax.shard_map(
        per_device, mesh=mesh, in_specs=placed, out_specs=P(("seq", "kvh"), None), check_vma=False
    )
```

```python
import functools
import math

import jax
import jax.numpy as jnp
from jax import lax
from jax.experimental import pallas as pl
from jax.sharding import PartitionSpec as P

BLOCK_TOKENS = 2048
BLOCK_PICK_LIMIT = 2
WINDOW_SHIFTS = (8, 4, 16, 2, 1)
LOG2_E = 1.4426950408889634


def shifted(value, axis, steps):
    count = lax.axis_size(axis)
    initial, last = (max(0, -steps), min(count, count - steps))
    return lax.ppermute(value, axis, [(source, source + steps) for source in range(initial, last)])


def gather_window(stretch_kv, span_devices, companions):
    stack = stretch_kv[None]
    offsets = [0]
    results = []
    for index, step in enumerate(WINDOW_SHIFTS):
        if len(offsets) >= span_devices:
            break
        arrived = shifted(stack, "seq", step)
        if index < len(companions) and companions[index] is not None:
            arrived, done = lax.optimization_barrier((arrived, companions[index]()))
            results.append(done)
        stack = jnp.concatenate([stack, arrived], axis=0)
        offsets = offsets + [o + step for o in offsets]
    return stack, offsets, results


def attend_kernel(masked, scaling, group_size, *refs):
    if masked:
        thr_ref, q_ref, k_ref, v_ref, o_ref, lse_ref = refs
    else:
        q_ref, k_ref, v_ref, o_ref, lse_ref = refs
    q = q_ref[...]
    q = q.reshape(-1, q.shape[-1])
    scores = lax.dot_general(
        q, k_ref[...], (((1,), (1,)), ((), ())), preferred_element_type=jnp.float32
    )
    if masked:
        token = lax.broadcasted_iota(jnp.int32, (scores.shape[0], 1), 0) // group_size
        scores = jnp.where(token >= thr_ref[...], scores, -jnp.inf)
    highest = jnp.max(scores, axis=1, keepdims=True)
    raw_weights = jnp.exp2((scores - highest) * (scaling * LOG2_E))
    weight_sum = jnp.sum(raw_weights, axis=1, keepdims=True)
    blended = (
        jnp.dot(raw_weights.astype(jnp.bfloat16), v_ref[...], preferred_element_type=jnp.float32)
        / weight_sum
    )
    o_ref[...] = blended.astype(o_ref.dtype).reshape(o_ref.shape)
    lse_ref[...] = highest * scaling + jnp.log(weight_sum)


def attend(q, q_block, q_map, heads, tiles, keys, values, out_dtype, scaling, group_size, thr=None, out_rows=None, out_map=None):
    rows = q_block[0] * q_block[-2] if len(q_block) == 4 else q_block[-2]
    total_rows = rows * tiles
    key_count, head_dim = keys.shape[1], keys.shape[2]
    kv_spec = pl.BlockSpec((None, key_count, head_dim), lambda h, i: (h, 0, 0))
    in_specs = [pl.BlockSpec(q_block, q_map), kv_spec, kv_spec]
    operands = [q, keys, values]
    if thr is not None:
        in_specs = [pl.BlockSpec((1, key_count), lambda h, i: (0, 0))] + in_specs
        operands = [thr] + operands
    cost = pl.CostEstimate(
        flops=4 * heads * total_rows * key_count * head_dim,
        transcendentals=heads * total_rows * key_count,
        bytes_accessed=2 * (2 * heads * total_rows * head_dim + 2 * heads * key_count * head_dim),
    )
    return pl.pallas_call(
        functools.partial(attend_kernel, thr is not None, scaling, group_size),
        grid=(heads, tiles),
        in_specs=in_specs,
        out_specs=[
            pl.BlockSpec(q_block, out_map or q_map),
            pl.BlockSpec((None, rows, 1), lambda h, i: (h, i, 0)),
        ],
        out_shape=[
            jax.ShapeDtypeStruct(((out_rows or q.shape[0]),) + q.shape[1:], out_dtype),
            jax.ShapeDtypeStruct((heads, total_rows, 1), jnp.float32),
        ],
        cost_estimate=cost,
    )(*operands)


def per_device(queries, stretch_kv, cache_kv, selection, block_owner):
    rows_local, query_heads, head_dim = queries.shape
    kv_heads = stretch_kv.shape[2]
    group_size = query_heads // kv_heads
    top_count = selection.shape[2]
    scaling = 1.0 / math.sqrt(head_dim)
    seq_count = lax.axis_size("seq")
    capacity = BLOCK_PICK_LIMIT
    span_devices = min(BLOCK_TOKENS // rows_local, seq_count)
    seq_place = lax.axis_index("seq")
    grouped = queries.reshape(rows_local, kv_heads, group_size, head_dim)
    requests = rows_local * top_count
    targets = block_owner[selection].reshape(kv_heads, requests)
    matches = (targets[:, :, None] == jnp.arange(seq_count, dtype=jnp.int32)[None, None, :]).astype(
        jnp.int32
    )
    places = jnp.sum((jnp.cumsum(matches, axis=1) - 1) * matches, axis=2)
    slots = targets * capacity + places
    one_hot = (
        (slots[:, None, :] == jnp.arange(seq_count * capacity, dtype=jnp.int32)[None, :, None])
        .astype(jnp.bfloat16)
        .reshape(kv_heads, seq_count, capacity, requests)
    )
    requested = jnp.repeat(jnp.swapaxes(grouped, 0, 1), top_count, axis=1).reshape(
        kv_heads, requests, group_size * head_dim
    )
    outgoing = jnp.einsum(
        "htcr,hrx->thcx", one_hot, requested, preferred_element_type=jnp.float32
    ).astype(jnp.bfloat16)
    slab = capacity * group_size
    outgoing = outgoing.reshape(seq_count, kv_heads, slab, head_dim)
    arrived = lax.all_to_all(outgoing, "seq", split_axis=0, concat_axis=0, tiled=True)
    arrived, window_start = lax.optimization_barrier((arrived, stretch_kv))
    cache_keys = jnp.swapaxes(cache_kv[0, 0], 0, 1)
    cache_values = jnp.swapaxes(cache_kv[1, 0], 0, 1)
    sources_per_tile = 32
    pieces = seq_count // sources_per_tile

    def serve_piece(piece):
        return attend(
            arrived,
            (sources_per_tile, None, slab, head_dim),
            lambda h, i: (piece, h, 0, 0),
            kv_heads,
            1,
            cache_keys,
            cache_values,
            jnp.bfloat16,
            scaling,
            group_size,
            out_rows=sources_per_tile,
            out_map=lambda h, i: (0, h, 0, 0),
        )

    window, offsets, served_pieces = gather_window(
        window_start,
        span_devices,
        [None] + [functools.partial(serve_piece, piece) for piece in range(pieces)],
    )
    blocks = window.shape[0]
    served = jnp.concatenate([piece[0] for piece in served_pieces], axis=0)
    served_lse = jnp.concatenate(
        [piece[1].reshape(kv_heads, sources_per_tile, slab) for piece in served_pieces], axis=1
    )
    served_lse = jnp.swapaxes(served_lse, 0, 1)
    served, served_lse, window = lax.optimization_barrier((served, served_lse, window))
    lse_rounded = lax.reduce_precision(served_lse, exponent_bits=8, mantissa_bits=7)
    lse_high = lse_rounded.astype(jnp.bfloat16)
    lse_low = (served_lse - lse_rounded).astype(jnp.bfloat16)
    payload_width = kv_heads * slab * head_dim
    lse_width = 2 * kv_heads * slab
    lse_lanes = -(-lse_width // 128) * 128
    lse_pack = jnp.concatenate([lse_high, lse_low], axis=2).reshape(seq_count, lse_width)
    payload = jnp.concatenate(
        [
            served.reshape(seq_count, payload_width),
            jnp.pad(lse_pack, ((0, 0), (0, lse_lanes - lse_width))),
        ],
        axis=1,
    )
    returned = lax.all_to_all(payload, "seq", split_axis=0, concat_axis=0, tiled=True)
    answers = returned[:, :payload_width].reshape(seq_count, kv_heads, capacity, group_size * head_dim)
    lse_parts = returned[:, payload_width : payload_width + lse_width].reshape(
        seq_count, kv_heads, 2 * slab
    ).astype(jnp.float32)
    answer_lse = (lse_parts[:, :, :slab] + lse_parts[:, :, slab:]).reshape(
        seq_count, kv_heads, capacity, group_size
    )
    window_keys = jnp.transpose(window[:, 0], (2, 0, 1, 3)).reshape(kv_heads, blocks * rows_local, head_dim)
    window_values = jnp.transpose(window[:, 1], (2, 0, 1, 3)).reshape(kv_heads, blocks * rows_local, head_dim)
    key_index = jnp.arange(blocks * rows_local, dtype=jnp.int32)
    key_offset = jnp.asarray(offsets, jnp.int32)[key_index // rows_local]
    threshold = jnp.where(
        seq_place - key_offset >= 0,
        jnp.where(key_offset == 0, key_index % rows_local, 0),
        rows_local,
    )[None, :]
    window_queries = jnp.swapaxes(grouped, 0, 1).reshape(kv_heads, rows_local * group_size, head_dim)
    own_out, own_lse = attend(
        window_queries,
        (None, rows_local * group_size, head_dim),
        lambda h, i: (h, 0, 0),
        kv_heads,
        1,
        window_keys,
        window_values,
        jnp.float32,
        scaling,
        group_size,
        threshold,
    )
    own_out = own_out.reshape(kv_heads, rows_local, group_size, head_dim)
    own_lse = own_lse.reshape(kv_heads, rows_local, group_size)
    head_rows = jnp.arange(kv_heads, dtype=jnp.int32)[:, None]
    picked = (
        jnp.einsum(
            "htcr,thcx->hrx",
            one_hot,
            answers,
            preferred_element_type=jnp.float32,
        )
        .reshape(kv_heads, rows_local, top_count, group_size, head_dim)
    )
    picked_lse = answer_lse[targets, head_rows, places].reshape(
        kv_heads, rows_local, top_count, group_size
    )
    ceiling = jnp.maximum(own_lse, jnp.max(picked_lse, axis=2))
    own_weight = jnp.exp(own_lse - ceiling)
    far_weight = jnp.exp(picked_lse - ceiling[:, :, None])
    denominator = own_weight + jnp.sum(far_weight, axis=2)
    combined = (
        own_weight[..., None] * own_out + jnp.sum(far_weight[..., None] * picked, axis=2)
    ) / denominator[..., None]
    heads_out = (
        jnp.transpose(combined, (1, 0, 2, 3))
        .astype(jnp.bfloat16)
        .reshape(rows_local, query_heads * head_dim)
    )
    return lax.all_to_all(heads_out, "kvh", split_axis=0, concat_axis=1, tiled=True)


def solution(mesh):
    placed = (
        P("seq", "kvh", None),
        P(None, "seq", "kvh", None),
        P(None, "seq", None, "kvh", None),
        P("kvh", "seq", None),
        P(),
    )
    return jax.shard_map(
        per_device, mesh=mesh, in_specs=placed, out_specs=P(("seq", "kvh"), None), check_vma=False
    )
```

```python
import functools
import math

import jax
import jax.numpy as jnp
from jax import lax
from jax.experimental import pallas as pl
from jax.sharding import PartitionSpec as P

BLOCK_TOKENS = 2048
BLOCK_PICK_LIMIT = 2
WINDOW_SHIFTS = (8, 4, 16, 2, 1)
LOG2_E = 1.4426950408889634


def shifted(value, axis, steps):
    count = lax.axis_size(axis)
    initial, last = (max(0, -steps), min(count, count - steps))
    return lax.ppermute(value, axis, [(source, source + steps) for source in range(initial, last)])


def gather_window(stretch_kv, span_devices, companions):
    stack = stretch_kv[None]
    offsets = [0]
    results = []
    for index, step in enumerate(WINDOW_SHIFTS):
        if len(offsets) >= span_devices:
            break
        arrived = shifted(stack, "seq", step)
        if index < len(companions) and companions[index] is not None:
            arrived, done = lax.optimization_barrier((arrived, companions[index]()))
            results.append(done)
        stack = jnp.concatenate([stack, arrived], axis=0)
        offsets = offsets + [o + step for o in offsets]
    return stack, offsets, results


def attend_kernel(masked, scaling, group_size, *refs):
    if masked:
        thr_ref, q_ref, k_ref, v_ref, o_ref, lse_ref = refs
    else:
        q_ref, k_ref, v_ref, o_ref, lse_ref = refs
    q = q_ref[...]
    q = q.reshape(-1, q.shape[-1])
    scores = lax.dot_general(
        q, k_ref[...], (((1,), (1,)), ((), ())), preferred_element_type=jnp.float32
    )
    if masked:
        token = lax.broadcasted_iota(jnp.int32, (scores.shape[0], 1), 0) // group_size
        scores = jnp.where(token >= thr_ref[...], scores, -jnp.inf)
    highest = jnp.max(scores, axis=1, keepdims=True)
    raw_weights = jnp.exp2((scores - highest) * (scaling * LOG2_E))
    weight_sum = jnp.sum(raw_weights, axis=1, keepdims=True)
    blended = (
        jnp.dot(raw_weights.astype(jnp.bfloat16), v_ref[...], preferred_element_type=jnp.float32)
        / weight_sum
    )
    o_ref[...] = blended.astype(o_ref.dtype).reshape(o_ref.shape)
    lse_ref[...] = highest * scaling + jnp.log(weight_sum)


def attend(q, q_block, q_map, heads, tiles, keys, values, out_dtype, scaling, group_size, thr=None, out_rows=None, out_map=None):
    rows = q_block[0] * q_block[-2] if len(q_block) == 4 else q_block[-2]
    total_rows = rows * tiles
    key_count, head_dim = keys.shape[1], keys.shape[2]
    kv_spec = pl.BlockSpec((None, key_count, head_dim), lambda h, i: (h, 0, 0))
    in_specs = [pl.BlockSpec(q_block, q_map), kv_spec, kv_spec]
    operands = [q, keys, values]
    if thr is not None:
        in_specs = [pl.BlockSpec((1, key_count), lambda h, i: (0, 0))] + in_specs
        operands = [thr] + operands
    cost = pl.CostEstimate(
        flops=4 * heads * total_rows * key_count * head_dim,
        transcendentals=heads * total_rows * key_count,
        bytes_accessed=2 * (2 * heads * total_rows * head_dim + 2 * heads * key_count * head_dim),
    )
    return pl.pallas_call(
        functools.partial(attend_kernel, thr is not None, scaling, group_size),
        grid=(heads, tiles),
        in_specs=in_specs,
        out_specs=[
            pl.BlockSpec(q_block, out_map or q_map),
            pl.BlockSpec((None, rows, 1), lambda h, i: (h, i, 0)),
        ],
        out_shape=[
            jax.ShapeDtypeStruct(((out_rows or q.shape[0]),) + q.shape[1:], out_dtype),
            jax.ShapeDtypeStruct((heads, total_rows, 1), jnp.float32),
        ],
        cost_estimate=cost,
    )(*operands)


def per_device(queries, stretch_kv, cache_kv, selection, block_owner):
    rows_local, query_heads, head_dim = queries.shape
    kv_heads = stretch_kv.shape[2]
    group_size = query_heads // kv_heads
    top_count = selection.shape[2]
    scaling = 1.0 / math.sqrt(head_dim)
    seq_count = lax.axis_size("seq")
    capacity = BLOCK_PICK_LIMIT
    span_devices = min(BLOCK_TOKENS // rows_local, seq_count)
    seq_place = lax.axis_index("seq")
    grouped = queries.reshape(rows_local, kv_heads, group_size, head_dim)
    requests = rows_local * top_count
    targets = block_owner[selection].reshape(kv_heads, requests)
    matches = (targets[:, :, None] == jnp.arange(seq_count, dtype=jnp.int32)[None, None, :]).astype(
        jnp.int32
    )
    places = jnp.sum((jnp.cumsum(matches, axis=1) - 1) * matches, axis=2)
    slots = targets * capacity + places
    one_hot = (
        (slots[:, None, :] == jnp.arange(seq_count * capacity, dtype=jnp.int32)[None, :, None])
        .astype(jnp.bfloat16)
        .reshape(kv_heads, seq_count, capacity, requests)
    )
    requested = jnp.repeat(jnp.swapaxes(grouped, 0, 1), top_count, axis=1).reshape(
        kv_heads, requests, group_size * head_dim
    )
    outgoing = jnp.einsum(
        "htcr,hrx->thcx", one_hot, requested, preferred_element_type=jnp.float32
    ).astype(jnp.bfloat16)
    slab = capacity * group_size
    outgoing = outgoing.reshape(seq_count, kv_heads, slab, head_dim)
    arrived = lax.all_to_all(outgoing, "seq", split_axis=0, concat_axis=0, tiled=True)
    arrived, window_start = lax.optimization_barrier((arrived, stretch_kv))
    cache_keys = jnp.swapaxes(cache_kv[0, 0], 0, 1)
    cache_values = jnp.swapaxes(cache_kv[1, 0], 0, 1)
    sources_per_tile = 32
    pieces = seq_count // sources_per_tile

    def serve_piece(piece):
        return attend(
            arrived[piece * sources_per_tile : (piece + 1) * sources_per_tile],
            (sources_per_tile, None, slab, head_dim),
            lambda h, i: (0, h, 0, 0),
            kv_heads,
            1,
            cache_keys,
            cache_values,
            jnp.bfloat16,
            scaling,
            group_size,
        )

    window, offsets, served_pieces = gather_window(
        window_start,
        span_devices,
        [None] + [functools.partial(serve_piece, piece) for piece in range(pieces)],
    )
    blocks = window.shape[0]
    served = jnp.concatenate([piece[0] for piece in served_pieces], axis=0)
    served_lse = jnp.concatenate(
        [piece[1].reshape(kv_heads, sources_per_tile, slab) for piece in served_pieces], axis=1
    )
    served_lse = jnp.swapaxes(served_lse, 0, 1)
    served, served_lse, window = lax.optimization_barrier((served, served_lse, window))
    lse_rounded = lax.reduce_precision(served_lse, exponent_bits=8, mantissa_bits=7)
    lse_high = lse_rounded.astype(jnp.bfloat16)
    lse_low = (served_lse - lse_rounded).astype(jnp.bfloat16)
    payload_width = kv_heads * slab * head_dim
    lse_width = 2 * kv_heads * slab
    lse_lanes = -(-lse_width // 128) * 128
    lse_pack = jnp.concatenate([lse_high, lse_low], axis=2).reshape(seq_count, lse_width)
    payload = jnp.concatenate(
        [
            served.reshape(seq_count, payload_width),
            jnp.pad(lse_pack, ((0, 0), (0, lse_lanes - lse_width))),
        ],
        axis=1,
    )
    returned = lax.all_to_all(payload, "seq", split_axis=0, concat_axis=0, tiled=True)
    answers = returned[:, :payload_width].reshape(seq_count, kv_heads, capacity, group_size * head_dim)
    lse_parts = returned[:, payload_width : payload_width + lse_width].reshape(
        seq_count, kv_heads, 2, capacity, group_size
    )
    lse_parts = jnp.swapaxes(lse_parts, 2, 3).reshape(seq_count, kv_heads, capacity, 2 * group_size)
    window_keys = jnp.transpose(window[:, 0], (2, 0, 1, 3)).reshape(kv_heads, blocks * rows_local, head_dim)
    window_values = jnp.transpose(window[:, 1], (2, 0, 1, 3)).reshape(kv_heads, blocks * rows_local, head_dim)
    key_index = jnp.arange(blocks * rows_local, dtype=jnp.int32)
    key_offset = jnp.asarray(offsets, jnp.int32)[key_index // rows_local]
    threshold = jnp.where(
        seq_place - key_offset >= 0,
        jnp.where(key_offset == 0, key_index % rows_local, 0),
        rows_local,
    )[None, :]
    window_queries = jnp.swapaxes(grouped, 0, 1).reshape(kv_heads, rows_local * group_size, head_dim)
    own_out, own_lse = attend(
        window_queries,
        (None, rows_local * group_size, head_dim),
        lambda h, i: (h, 0, 0),
        kv_heads,
        1,
        window_keys,
        window_values,
        jnp.float32,
        scaling,
        group_size,
        threshold,
    )
    own_out = own_out.reshape(kv_heads, rows_local, group_size, head_dim)
    own_lse = own_lse.reshape(kv_heads, rows_local, group_size)
    head_rows = jnp.arange(kv_heads, dtype=jnp.int32)[:, None]
    picked = (
        jnp.einsum(
            "htcr,thcx->hrx",
            one_hot,
            answers,
            preferred_element_type=jnp.float32,
        )
        .reshape(kv_heads, rows_local, top_count, group_size, head_dim)
    )
    picked_parts = jnp.einsum(
        "htcr,thcx->hrx", one_hot, lse_parts, preferred_element_type=jnp.float32
    )
    picked_lse = (picked_parts[..., :group_size] + picked_parts[..., group_size:]).reshape(
        kv_heads, rows_local, top_count, group_size
    )
    ceiling = jnp.maximum(own_lse, jnp.max(picked_lse, axis=2))
    own_weight = jnp.exp(own_lse - ceiling)
    far_weight = jnp.exp(picked_lse - ceiling[:, :, None])
    denominator = own_weight + jnp.sum(far_weight, axis=2)
    combined = (
        own_weight[..., None] * own_out + jnp.sum(far_weight[..., None] * picked, axis=2)
    ) / denominator[..., None]
    heads_out = (
        jnp.transpose(combined, (1, 0, 2, 3))
        .astype(jnp.bfloat16)
        .reshape(rows_local, query_heads * head_dim)
    )
    return lax.all_to_all(heads_out, "kvh", split_axis=0, concat_axis=1, tiled=True)


def solution(mesh):
    placed = (
        P("seq", "kvh", None),
        P(None, "seq", "kvh", None),
        P(None, "seq", None, "kvh", None),
        P("kvh", "seq", None),
        P(),
    )
    return jax.shard_map(
        per_device, mesh=mesh, in_specs=placed, out_specs=P(("seq", "kvh"), None), check_vma=False
    )
```

```python
import functools
import math

import jax
import jax.numpy as jnp
from jax import lax
from jax.experimental import pallas as pl
from jax.sharding import Mesh, PartitionSpec as P

BLOCK_TOKENS = 2048
STRETCH_TOKENS = 8192
SEQ = ("seq_group", "seq_slot")
BLOCK_PICK_LIMIT = 2
LOG2_E = 1.4426950408889634


def shifted(value, axis, steps, count):
    initial, last = (max(0, -steps), min(count, count - steps))
    return lax.ppermute(value, axis, [(source, source + steps) for source in range(initial, last)])


def attend_kernel(masked, scaling, group_size, *refs):
    if masked:
        thr_ref, q_ref, k_ref, v_ref, o_ref, lse_ref = refs
    else:
        q_ref, k_ref, v_ref, o_ref, lse_ref = refs
    q = q_ref[...]
    q = q.reshape(-1, q.shape[-1])
    scores = lax.dot_general(
        q, k_ref[...], (((1,), (1,)), ((), ())), preferred_element_type=jnp.float32
    )
    if masked:
        token = lax.broadcasted_iota(jnp.int32, (scores.shape[0], 1), 0) // group_size
        scores = jnp.where(token >= thr_ref[...], scores, -jnp.inf)
    highest = jnp.max(scores, axis=1, keepdims=True)
    raw_weights = jnp.exp2((scores - highest) * (scaling * LOG2_E))
    weight_sum = jnp.sum(raw_weights, axis=1, keepdims=True)
    blended = (
        jnp.dot(raw_weights.astype(jnp.bfloat16), v_ref[...], preferred_element_type=jnp.float32)
        / weight_sum
    )
    o_ref[...] = blended.astype(o_ref.dtype).reshape(o_ref.shape)
    lse_ref[...] = highest * scaling + jnp.log(weight_sum)


def attend(q, q_block, q_map, heads, tiles, keys, values, out_dtype, scaling, group_size, thr=None, out_rows=None, out_map=None):
    rows = q_block[0] * q_block[-2] if len(q_block) == 4 else q_block[-2]
    total_rows = rows * tiles
    key_count, head_dim = keys.shape[1], keys.shape[2]
    kv_spec = pl.BlockSpec((None, key_count, head_dim), lambda h, i: (h, 0, 0))
    in_specs = [pl.BlockSpec(q_block, q_map), kv_spec, kv_spec]
    operands = [q, keys, values]
    if thr is not None:
        in_specs = [pl.BlockSpec((1, key_count), lambda h, i: (0, 0))] + in_specs
        operands = [thr] + operands
    cost = pl.CostEstimate(
        flops=4 * heads * total_rows * key_count * head_dim,
        transcendentals=heads * total_rows * key_count,
        bytes_accessed=2 * (2 * heads * total_rows * head_dim + 2 * heads * key_count * head_dim),
    )
    return pl.pallas_call(
        functools.partial(attend_kernel, thr is not None, scaling, group_size),
        grid=(heads, tiles),
        in_specs=in_specs,
        out_specs=[
            pl.BlockSpec(q_block, out_map or q_map),
            pl.BlockSpec((None, rows, 1), lambda h, i: (h, i, 0)),
        ],
        out_shape=[
            jax.ShapeDtypeStruct(((out_rows or q.shape[0]),) + q.shape[1:], out_dtype),
            jax.ShapeDtypeStruct((heads, total_rows, 1), jnp.float32),
        ],
        cost_estimate=cost,
    )(*operands)


def per_device(queries, stretch_kv, cache_kv, selection, block_owner):
    rows_local, query_heads, head_dim = queries.shape
    kv_heads = stretch_kv.shape[2]
    group_size = query_heads // kv_heads
    top_count = selection.shape[2]
    scaling = 1.0 / math.sqrt(head_dim)
    group_count, window_group = lax.axis_size("seq_group"), lax.axis_size("seq_slot")
    seq_count = group_count * window_group
    capacity = BLOCK_PICK_LIMIT
    span_devices = min(BLOCK_TOKENS // rows_local, seq_count)
    slot_place = lax.axis_index("seq_slot")
    seq_place = lax.axis_index("seq_group") * window_group + slot_place
    grouped = queries.reshape(rows_local, kv_heads, group_size, head_dim)
    requests = rows_local * top_count
    targets = block_owner[selection].reshape(kv_heads, requests)
    matches = (targets[:, :, None] == jnp.arange(seq_count, dtype=jnp.int32)[None, None, :]).astype(
        jnp.int32
    )
    places = jnp.sum((jnp.cumsum(matches, axis=1) - 1) * matches, axis=2)
    slots = targets * capacity + places
    one_hot = (
        (slots[:, None, :] == jnp.arange(seq_count * capacity, dtype=jnp.int32)[None, :, None])
        .astype(jnp.bfloat16)
        .reshape(kv_heads, seq_count, capacity, requests)
    )
    requested = jnp.repeat(jnp.swapaxes(grouped, 0, 1), top_count, axis=1).reshape(
        kv_heads, requests, group_size * head_dim
    )
    outgoing = jnp.einsum(
        "htcr,hrx->thcx", one_hot, requested, preferred_element_type=jnp.float32
    ).astype(jnp.bfloat16)
    slab = capacity * group_size
    outgoing = outgoing.reshape(seq_count, kv_heads, slab, head_dim)
    arrived = lax.all_to_all(outgoing, SEQ, split_axis=0, concat_axis=0, tiled=True)
    earlier = shifted(stretch_kv, SEQ, window_group, seq_count)
    gathered_earlier = lax.all_gather(earlier, "seq_slot", axis=0, tiled=False)
    gathered_own = lax.all_gather(stretch_kv, "seq_slot", axis=0, tiled=False)
    cache_keys = jnp.swapaxes(cache_kv[0, 0], 0, 1)
    cache_values = jnp.swapaxes(cache_kv[1, 0], 0, 1)
    sources_per_tile = 32
    served, served_lse = attend(
        arrived,
        (sources_per_tile, None, slab, head_dim),
        lambda h, i: (i, h, 0, 0),
        kv_heads,
        seq_count // sources_per_tile,
        cache_keys,
        cache_values,
        jnp.bfloat16,
        scaling,
        group_size,
    )
    served_lse = jnp.swapaxes(served_lse.reshape(kv_heads, seq_count, slab), 0, 1)
    both = jnp.concatenate([gathered_earlier, gathered_own], axis=0)
    window = lax.dynamic_slice_in_dim(both, slot_place + window_group - span_devices + 1, span_devices, 0)
    offsets = [span_devices - 1 - p for p in range(span_devices)]
    blocks = window.shape[0]
    lse_rounded = lax.reduce_precision(served_lse, exponent_bits=8, mantissa_bits=7)
    lse_high = lse_rounded.astype(jnp.bfloat16)
    lse_low = (served_lse - lse_rounded).astype(jnp.bfloat16)
    payload_width = kv_heads * slab * head_dim
    lse_width = 2 * kv_heads * slab
    lse_lanes = -(-lse_width // 128) * 128
    lse_pack = jnp.concatenate([lse_high, lse_low], axis=2).reshape(seq_count, lse_width)
    payload = jnp.concatenate(
        [
            served.reshape(seq_count, payload_width),
            jnp.pad(lse_pack, ((0, 0), (0, lse_lanes - lse_width))),
        ],
        axis=1,
    )
    returned = lax.all_to_all(payload, SEQ, split_axis=0, concat_axis=0, tiled=True)
    answers = returned[:, :payload_width].reshape(seq_count, kv_heads, capacity, group_size * head_dim)
    lse_parts = returned[:, payload_width : payload_width + lse_width].reshape(
        seq_count, kv_heads, 2, capacity, group_size
    )
    lse_parts = jnp.swapaxes(lse_parts, 2, 3).reshape(seq_count, kv_heads, capacity, 2 * group_size)
    window_keys = jnp.transpose(window[:, 0], (2, 0, 1, 3)).reshape(kv_heads, blocks * rows_local, head_dim)
    window_values = jnp.transpose(window[:, 1], (2, 0, 1, 3)).reshape(kv_heads, blocks * rows_local, head_dim)
    key_index = jnp.arange(blocks * rows_local, dtype=jnp.int32)
    key_offset = jnp.asarray(offsets, jnp.int32)[key_index // rows_local]
    threshold = jnp.where(
        seq_place - key_offset >= 0,
        jnp.where(key_offset == 0, key_index % rows_local, 0),
        rows_local,
    )[None, :]
    window_queries = jnp.swapaxes(grouped, 0, 1).reshape(kv_heads, rows_local * group_size, head_dim)
    own_out, own_lse = attend(
        window_queries,
        (None, rows_local * group_size, head_dim),
        lambda h, i: (h, 0, 0),
        kv_heads,
        1,
        window_keys,
        window_values,
        jnp.float32,
        scaling,
        group_size,
        threshold,
    )
    own_out = own_out.reshape(kv_heads, rows_local, group_size, head_dim)
    own_lse = own_lse.reshape(kv_heads, rows_local, group_size)
    head_rows = jnp.arange(kv_heads, dtype=jnp.int32)[:, None]
    picked = (
        jnp.einsum(
            "htcr,thcx->hrx",
            one_hot,
            answers,
            preferred_element_type=jnp.float32,
        )
        .reshape(kv_heads, rows_local, top_count, group_size, head_dim)
    )
    picked_parts = jnp.einsum(
        "htcr,thcx->hrx", one_hot, lse_parts, preferred_element_type=jnp.float32
    )
    picked_lse = (picked_parts[..., :group_size] + picked_parts[..., group_size:]).reshape(
        kv_heads, rows_local, top_count, group_size
    )
    ceiling = jnp.maximum(own_lse, jnp.max(picked_lse, axis=2))
    own_weight = jnp.exp(own_lse - ceiling)
    far_weight = jnp.exp(picked_lse - ceiling[:, :, None])
    denominator = own_weight + jnp.sum(far_weight, axis=2)
    combined = (
        own_weight[..., None] * own_out + jnp.sum(far_weight[..., None] * picked, axis=2)
    ) / denominator[..., None]
    heads_out = (
        jnp.transpose(combined, (1, 0, 2, 3))
        .astype(jnp.bfloat16)
        .reshape(rows_local, query_heads * head_dim)
    )
    return lax.all_to_all(heads_out, "kvh", split_axis=0, concat_axis=1, tiled=True)


def solution(mesh):
    seq_total, kvh_total = mesh.devices.shape
    window_group = min(BLOCK_TOKENS // (STRETCH_TOKENS // seq_total), seq_total)
    split_mesh = Mesh(
        mesh.devices.reshape(seq_total // window_group, window_group, kvh_total),
        ("seq_group", "seq_slot", "kvh"),
    )
    placed = (
        P(SEQ, "kvh", None),
        P(None, SEQ, "kvh", None),
        P(None, SEQ, None, "kvh", None),
        P("kvh", SEQ, None),
        P(),
    )
    return jax.shard_map(
        per_device,
        mesh=split_mesh,
        in_specs=placed,
        out_specs=P(SEQ + ("kvh",), None),
        check_vma=False,
    )
```

```python
import functools
import math

import jax
import jax.numpy as jnp
from jax import lax
from jax.experimental import pallas as pl
from jax.sharding import PartitionSpec as P

BLOCK_TOKENS = 2048
BLOCK_PICK_LIMIT = 2
WINDOW_SHIFTS = (8, 4, 16, 2, 1)
LOG2_E = 1.4426950408889634


def shifted(value, axis, steps):
    count = lax.axis_size(axis)
    initial, last = (max(0, -steps), min(count, count - steps))
    return lax.ppermute(value, axis, [(source, source + steps) for source in range(initial, last)])


def gather_window(stretch_kv, span_devices, partner, meet_step, companions):
    stack = stretch_kv[None]
    offsets = [0]
    results = []
    for index, step in enumerate(WINDOW_SHIFTS):
        if len(offsets) >= span_devices:
            break
        arrived = shifted(stack, "seq", step)
        if index == meet_step:
            arrived, partner = lax.optimization_barrier((arrived, partner))
        if companions[index] is not None:
            arrived, done = lax.optimization_barrier((arrived, companions[index](partner)))
            results.extend(done)
        stack = jnp.concatenate([stack, arrived], axis=0)
        offsets = offsets + [o + step for o in offsets]
    return stack, offsets, results


def attend_kernel(masked, scaling, group_size, *refs):
    if masked:
        thr_ref, q_ref, k_ref, v_ref, o_ref, lse_ref = refs
    else:
        q_ref, k_ref, v_ref, o_ref, lse_ref = refs
    q = q_ref[...]
    q = q.reshape(-1, q.shape[-1])
    scores = lax.dot_general(
        q, k_ref[...], (((1,), (1,)), ((), ())), preferred_element_type=jnp.float32
    )
    if masked:
        token = lax.broadcasted_iota(jnp.int32, (scores.shape[0], 1), 0) // group_size
        scores = jnp.where(token >= thr_ref[...], scores, -jnp.inf)
    highest = jnp.max(scores, axis=1, keepdims=True)
    raw_weights = jnp.exp2((scores - highest) * (scaling * LOG2_E))
    weight_sum = jnp.sum(raw_weights, axis=1, keepdims=True)
    blended = (
        jnp.dot(raw_weights.astype(jnp.bfloat16), v_ref[...], preferred_element_type=jnp.float32)
        / weight_sum
    )
    o_ref[...] = blended.astype(o_ref.dtype).reshape(o_ref.shape)
    lse_ref[...] = highest * scaling + jnp.log(weight_sum)


def attend(q, q_block, q_map, heads, tiles, keys, values, out_dtype, scaling, group_size, thr=None, out_rows=None, out_map=None):
    rows = q_block[0] * q_block[-2] if len(q_block) == 4 else q_block[-2]
    total_rows = rows * tiles
    key_count, head_dim = keys.shape[1], keys.shape[2]
    kv_spec = pl.BlockSpec((None, key_count, head_dim), lambda h, i: (h, 0, 0))
    in_specs = [pl.BlockSpec(q_block, q_map), kv_spec, kv_spec]
    operands = [q, keys, values]
    if thr is not None:
        in_specs = [pl.BlockSpec((1, key_count), lambda h, i: (0, 0))] + in_specs
        operands = [thr] + operands
    cost = pl.CostEstimate(
        flops=4 * heads * total_rows * key_count * head_dim,
        transcendentals=heads * total_rows * key_count,
        bytes_accessed=2 * (2 * heads * total_rows * head_dim + 2 * heads * key_count * head_dim),
    )
    return pl.pallas_call(
        functools.partial(attend_kernel, thr is not None, scaling, group_size),
        grid=(heads, tiles),
        in_specs=in_specs,
        out_specs=[
            pl.BlockSpec(q_block, out_map or q_map),
            pl.BlockSpec((None, rows, 1), lambda h, i: (h, i, 0)),
        ],
        out_shape=[
            jax.ShapeDtypeStruct(((out_rows or q.shape[0]),) + q.shape[1:], out_dtype),
            jax.ShapeDtypeStruct((heads, total_rows, 1), jnp.float32),
        ],
        cost_estimate=cost,
    )(*operands)


def per_device(queries, stretch_kv, cache_kv, selection, block_owner):
    rows_local, query_heads, head_dim = queries.shape
    kv_heads = stretch_kv.shape[2]
    group_size = query_heads // kv_heads
    top_count = selection.shape[2]
    scaling = 1.0 / math.sqrt(head_dim)
    seq_count = lax.axis_size("seq")
    capacity = BLOCK_PICK_LIMIT
    span_devices = min(BLOCK_TOKENS // rows_local, seq_count)
    seq_place = lax.axis_index("seq")
    grouped = queries.reshape(rows_local, kv_heads, group_size, head_dim)
    requests = rows_local * top_count
    targets = block_owner[selection].reshape(kv_heads, requests)
    matches = (targets[:, :, None] == jnp.arange(seq_count, dtype=jnp.int32)[None, None, :]).astype(
        jnp.int32
    )
    places = jnp.sum((jnp.cumsum(matches, axis=1) - 1) * matches, axis=2)
    slots = targets * capacity + places
    one_hot = (
        (slots[:, None, :] == jnp.arange(seq_count * capacity, dtype=jnp.int32)[None, :, None])
        .astype(jnp.bfloat16)
        .reshape(kv_heads, seq_count, capacity, requests)
    )
    requested = jnp.repeat(jnp.swapaxes(grouped, 0, 1), top_count, axis=1).reshape(
        kv_heads, requests, group_size * head_dim
    )
    outgoing = jnp.einsum(
        "htcr,hrx->thcx", one_hot, requested, preferred_element_type=jnp.float32
    ).astype(jnp.bfloat16)
    slab = capacity * group_size
    outgoing = outgoing.reshape(seq_count, kv_heads, slab, head_dim)
    arrived = lax.all_to_all(outgoing, "seq", split_axis=0, concat_axis=0, tiled=True)
    cache_keys = jnp.swapaxes(cache_kv[0, 0], 0, 1)
    cache_values = jnp.swapaxes(cache_kv[1, 0], 0, 1)
    sources_per_tile = 32
    pieces = seq_count // sources_per_tile

    def serve_piece(piece, arrived):
        return attend(
            arrived[piece * sources_per_tile : (piece + 1) * sources_per_tile],
            (sources_per_tile, None, slab, head_dim),
            lambda h, i: (0, h, 0, 0),
            kv_heads,
            1,
            cache_keys,
            cache_values,
            jnp.bfloat16,
            scaling,
            group_size,
        )

    def serve_pieces(first, last, arrived):
        return tuple(serve_piece(piece, arrived) for piece in range(first, last))

    window, offsets, served_pieces = gather_window(
        stretch_kv,
        span_devices,
        arrived,
        2,
        [None, None, None, functools.partial(serve_pieces, 0, pieces // 2),
         functools.partial(serve_pieces, pieces // 2, pieces)],
    )
    blocks = window.shape[0]
    served = jnp.concatenate([piece[0] for piece in served_pieces], axis=0)
    served_lse = jnp.concatenate(
        [piece[1].reshape(kv_heads, sources_per_tile, slab) for piece in served_pieces], axis=1
    )
    served_lse = jnp.swapaxes(served_lse, 0, 1)
    served, served_lse, window = lax.optimization_barrier((served, served_lse, window))
    lse_rounded = lax.reduce_precision(served_lse, exponent_bits=8, mantissa_bits=7)
    lse_high = lse_rounded.astype(jnp.bfloat16)
    lse_low = (served_lse - lse_rounded).astype(jnp.bfloat16)
    payload_width = kv_heads * slab * head_dim
    lse_width = 2 * kv_heads * slab
    lse_lanes = -(-lse_width // 128) * 128
    lse_pack = jnp.concatenate([lse_high, lse_low], axis=2).reshape(seq_count, lse_width)
    payload = jnp.concatenate(
        [
            served.reshape(seq_count, payload_width),
            jnp.pad(lse_pack, ((0, 0), (0, lse_lanes - lse_width))),
        ],
        axis=1,
    )
    returned = lax.all_to_all(payload, "seq", split_axis=0, concat_axis=0, tiled=True)
    answers = returned[:, :payload_width].reshape(seq_count, kv_heads, capacity, group_size * head_dim)
    lse_parts = returned[:, payload_width : payload_width + lse_width].reshape(
        seq_count, kv_heads, 2, capacity, group_size
    )
    lse_parts = jnp.swapaxes(lse_parts, 2, 3).reshape(seq_count, kv_heads, capacity, 2 * group_size)
    window_keys = jnp.transpose(window[:, 0], (2, 0, 1, 3)).reshape(kv_heads, blocks * rows_local, head_dim)
    window_values = jnp.transpose(window[:, 1], (2, 0, 1, 3)).reshape(kv_heads, blocks * rows_local, head_dim)
    key_index = jnp.arange(blocks * rows_local, dtype=jnp.int32)
    key_offset = jnp.asarray(offsets, jnp.int32)[key_index // rows_local]
    threshold = jnp.where(
        seq_place - key_offset >= 0,
        jnp.where(key_offset == 0, key_index % rows_local, 0),
        rows_local,
    )[None, :]
    window_queries = jnp.swapaxes(grouped, 0, 1).reshape(kv_heads, rows_local * group_size, head_dim)
    own_out, own_lse = attend(
        window_queries,
        (None, rows_local * group_size, head_dim),
        lambda h, i: (h, 0, 0),
        kv_heads,
        1,
        window_keys,
        window_values,
        jnp.float32,
        scaling,
        group_size,
        threshold,
    )
    own_out = own_out.reshape(kv_heads, rows_local, group_size, head_dim)
    own_lse = own_lse.reshape(kv_heads, rows_local, group_size)
    head_rows = jnp.arange(kv_heads, dtype=jnp.int32)[:, None]
    picked = (
        jnp.einsum(
            "htcr,thcx->hrx",
            one_hot,
            answers,
            preferred_element_type=jnp.float32,
        )
        .reshape(kv_heads, rows_local, top_count, group_size, head_dim)
    )
    picked_parts = jnp.einsum(
        "htcr,thcx->hrx", one_hot, lse_parts, preferred_element_type=jnp.float32
    )
    picked_lse = (picked_parts[..., :group_size] + picked_parts[..., group_size:]).reshape(
        kv_heads, rows_local, top_count, group_size
    )
    ceiling = jnp.maximum(own_lse, jnp.max(picked_lse, axis=2))
    own_weight = jnp.exp(own_lse - ceiling)
    far_weight = jnp.exp(picked_lse - ceiling[:, :, None])
    denominator = own_weight + jnp.sum(far_weight, axis=2)
    combined = (
        own_weight[..., None] * own_out + jnp.sum(far_weight[..., None] * picked, axis=2)
    ) / denominator[..., None]
    heads_out = (
        jnp.transpose(combined, (1, 0, 2, 3))
        .astype(jnp.bfloat16)
        .reshape(rows_local, query_heads * head_dim)
    )
    return lax.all_to_all(heads_out, "kvh", split_axis=0, concat_axis=1, tiled=True)


def solution(mesh):
    placed = (
        P("seq", "kvh", None),
        P(None, "seq", "kvh", None),
        P(None, "seq", None, "kvh", None),
        P("kvh", "seq", None),
        P(),
    )
    return jax.shard_map(
        per_device, mesh=mesh, in_specs=placed, out_specs=P(("seq", "kvh"), None), check_vma=False
    )
```

```python
import functools
import math

import jax
import jax.numpy as jnp
from jax import lax
from jax.experimental import pallas as pl
from jax.sharding import PartitionSpec as P

BLOCK_TOKENS = 2048
BLOCK_PICK_LIMIT = 2
WINDOW_SHIFTS = (8, 4, 16, 2, 1)
LOG2_E = 1.4426950408889634


def shifted(value, axis, steps):
    count = lax.axis_size(axis)
    initial, last = (max(0, -steps), min(count, count - steps))
    return lax.ppermute(value, axis, [(source, source + steps) for source in range(initial, last)])


def gather_window(stretch_kv, span_devices, companions):
    stack = stretch_kv[None]
    offsets = [0]
    results = []
    for index, step in enumerate(WINDOW_SHIFTS):
        if len(offsets) >= span_devices:
            break
        arrived = shifted(stack, "seq", step)
        if index < len(companions) and companions[index] is not None:
            arrived, done = lax.optimization_barrier((arrived, companions[index]()))
            results.append(done)
        stack = jnp.concatenate([stack, arrived], axis=0)
        offsets = offsets + [o + step for o in offsets]
    return stack, offsets, results


def attend_kernel(masked, scaling, group_size, *refs):
    if masked:
        thr_ref, q_ref, k_ref, v_ref, o_ref, lse_ref = refs
    else:
        q_ref, k_ref, v_ref, o_ref, lse_ref = refs
    q = q_ref[...]
    q = q.reshape(-1, q.shape[-1])
    scores = lax.dot_general(
        q, k_ref[...], (((1,), (1,)), ((), ())), preferred_element_type=jnp.float32
    )
    if masked:
        token = lax.broadcasted_iota(jnp.int32, (scores.shape[0], 1), 0) // group_size
        scores = jnp.where(token >= thr_ref[...], scores, -jnp.inf)
    highest = jnp.max(scores, axis=1, keepdims=True)
    raw_weights = jnp.exp2((scores - highest) * (scaling * LOG2_E))
    weight_sum = jnp.sum(raw_weights, axis=1, keepdims=True)
    blended = (
        jnp.dot(raw_weights.astype(jnp.bfloat16), v_ref[...], preferred_element_type=jnp.float32)
        / weight_sum
    )
    o_ref[...] = blended.astype(o_ref.dtype).reshape(o_ref.shape)
    log_sum = highest * scaling + jnp.log(weight_sum)
    lse_ref[...] = jnp.transpose(jnp.broadcast_to(log_sum, (log_sum.shape[0], 128)))[:8]


def attend(q, q_block, q_map, heads, tiles, keys, values, out_dtype, scaling, group_size, thr=None, out_rows=None, out_map=None):
    rows = q_block[0] * q_block[-2] if len(q_block) == 4 else q_block[-2]
    total_rows = rows * tiles
    key_count, head_dim = keys.shape[1], keys.shape[2]
    kv_spec = pl.BlockSpec((None, key_count, head_dim), lambda h, i: (h, 0, 0))
    in_specs = [pl.BlockSpec(q_block, q_map), kv_spec, kv_spec]
    operands = [q, keys, values]
    if thr is not None:
        in_specs = [pl.BlockSpec((1, key_count), lambda h, i: (0, 0))] + in_specs
        operands = [thr] + operands
    cost = pl.CostEstimate(
        flops=4 * heads * total_rows * key_count * head_dim,
        transcendentals=heads * total_rows * key_count,
        bytes_accessed=2 * (2 * heads * total_rows * head_dim + 2 * heads * key_count * head_dim),
    )
    return pl.pallas_call(
        functools.partial(attend_kernel, thr is not None, scaling, group_size),
        grid=(heads, tiles),
        in_specs=in_specs,
        out_specs=[
            pl.BlockSpec(q_block, out_map or q_map),
            pl.BlockSpec((None, None, 8, rows), lambda h, i: (h, i, 0, 0)),
        ],
        out_shape=[
            jax.ShapeDtypeStruct(((out_rows or q.shape[0]),) + q.shape[1:], out_dtype),
            jax.ShapeDtypeStruct((heads, tiles, 8, rows), jnp.float32),
        ],
        cost_estimate=cost,
    )(*operands)


def per_device(queries, stretch_kv, cache_kv, selection, block_owner):
    rows_local, query_heads, head_dim = queries.shape
    kv_heads = stretch_kv.shape[2]
    group_size = query_heads // kv_heads
    top_count = selection.shape[2]
    scaling = 1.0 / math.sqrt(head_dim)
    seq_count = lax.axis_size("seq")
    capacity = BLOCK_PICK_LIMIT
    span_devices = min(BLOCK_TOKENS // rows_local, seq_count)
    seq_place = lax.axis_index("seq")
    grouped = queries.reshape(rows_local, kv_heads, group_size, head_dim)
    requests = rows_local * top_count
    targets = block_owner[selection].reshape(kv_heads, requests)
    matches = (targets[:, :, None] == jnp.arange(seq_count, dtype=jnp.int32)[None, None, :]).astype(
        jnp.int32
    )
    places = jnp.sum((jnp.cumsum(matches, axis=1) - 1) * matches, axis=2)
    slots = targets * capacity + places
    one_hot = (
        (slots[:, None, :] == jnp.arange(seq_count * capacity, dtype=jnp.int32)[None, :, None])
        .astype(jnp.bfloat16)
        .reshape(kv_heads, seq_count, capacity, requests)
    )
    requested = jnp.repeat(jnp.swapaxes(grouped, 0, 1), top_count, axis=1).reshape(
        kv_heads, requests, group_size * head_dim
    )
    outgoing = jnp.einsum(
        "htcr,hrx->thcx", one_hot, requested, preferred_element_type=jnp.float32
    ).astype(jnp.bfloat16)
    slab = capacity * group_size
    outgoing = outgoing.reshape(seq_count, kv_heads, slab, head_dim)
    arrived = lax.all_to_all(outgoing, "seq", split_axis=0, concat_axis=0, tiled=True)
    arrived, window_start = lax.optimization_barrier((arrived, stretch_kv))
    cache_keys = jnp.swapaxes(cache_kv[0, 0], 0, 1)
    cache_values = jnp.swapaxes(cache_kv[1, 0], 0, 1)
    sources_per_tile = 32
    pieces = seq_count // sources_per_tile

    def serve_piece(piece):
        return attend(
            arrived[piece * sources_per_tile : (piece + 1) * sources_per_tile],
            (sources_per_tile, None, slab, head_dim),
            lambda h, i: (0, h, 0, 0),
            kv_heads,
            1,
            cache_keys,
            cache_values,
            jnp.bfloat16,
            scaling,
            group_size,
        )

    window, offsets, served_pieces = gather_window(
        window_start,
        span_devices,
        [None] + [functools.partial(serve_piece, piece) for piece in range(pieces)],
    )
    blocks = window.shape[0]
    served = jnp.concatenate([piece[0] for piece in served_pieces], axis=0)
    served_lse = jnp.concatenate(
        [piece[1][:, :, 0].reshape(kv_heads, sources_per_tile, slab) for piece in served_pieces], axis=1
    )
    served_lse = jnp.swapaxes(served_lse, 0, 1)
    served, served_lse, window = lax.optimization_barrier((served, served_lse, window))
    lse_rounded = lax.reduce_precision(served_lse, exponent_bits=8, mantissa_bits=7)
    lse_high = lse_rounded.astype(jnp.bfloat16)
    lse_low = (served_lse - lse_rounded).astype(jnp.bfloat16)
    payload_width = kv_heads * slab * head_dim
    lse_width = 2 * kv_heads * slab
    lse_lanes = -(-lse_width // 128) * 128
    lse_pack = jnp.concatenate([lse_high, lse_low], axis=2).reshape(seq_count, lse_width)
    payload = jnp.concatenate(
        [
            served.reshape(seq_count, payload_width),
            jnp.pad(lse_pack, ((0, 0), (0, lse_lanes - lse_width))),
        ],
        axis=1,
    )
    returned = lax.all_to_all(payload, "seq", split_axis=0, concat_axis=0, tiled=True)
    answers = returned[:, :payload_width].reshape(seq_count, kv_heads, capacity, group_size * head_dim)
    lse_parts = returned[:, payload_width : payload_width + lse_width].reshape(
        seq_count, kv_heads, 2, capacity, group_size
    )
    lse_parts = jnp.swapaxes(lse_parts, 2, 3).reshape(seq_count, kv_heads, capacity, 2 * group_size)
    window_keys = jnp.transpose(window[:, 0], (2, 0, 1, 3)).reshape(kv_heads, blocks * rows_local, head_dim)
    window_values = jnp.transpose(window[:, 1], (2, 0, 1, 3)).reshape(kv_heads, blocks * rows_local, head_dim)
    key_index = jnp.arange(blocks * rows_local, dtype=jnp.int32)
    key_offset = jnp.asarray(offsets, jnp.int32)[key_index // rows_local]
    threshold = jnp.where(
        seq_place - key_offset >= 0,
        jnp.where(key_offset == 0, key_index % rows_local, 0),
        rows_local,
    )[None, :]
    window_queries = jnp.swapaxes(grouped, 0, 1).reshape(kv_heads, rows_local * group_size, head_dim)
    own_out, own_lse = attend(
        window_queries,
        (None, rows_local * group_size, head_dim),
        lambda h, i: (h, 0, 0),
        kv_heads,
        1,
        window_keys,
        window_values,
        jnp.float32,
        scaling,
        group_size,
        threshold,
    )
    own_out = own_out.reshape(kv_heads, rows_local, group_size, head_dim)
    own_lse = own_lse[:, :, 0].reshape(kv_heads, rows_local, group_size)
    head_rows = jnp.arange(kv_heads, dtype=jnp.int32)[:, None]
    picked = (
        jnp.einsum(
            "htcr,thcx->hrx",
            one_hot,
            answers,
            preferred_element_type=jnp.float32,
        )
        .reshape(kv_heads, rows_local, top_count, group_size, head_dim)
    )
    picked_parts = jnp.einsum(
        "htcr,thcx->hrx", one_hot, lse_parts, preferred_element_type=jnp.float32
    )
    picked_lse = (picked_parts[..., :group_size] + picked_parts[..., group_size:]).reshape(
        kv_heads, rows_local, top_count, group_size
    )
    ceiling = jnp.maximum(own_lse, jnp.max(picked_lse, axis=2))
    own_weight = jnp.exp(own_lse - ceiling)
    far_weight = jnp.exp(picked_lse - ceiling[:, :, None])
    denominator = own_weight + jnp.sum(far_weight, axis=2)
    combined = (
        own_weight[..., None] * own_out + jnp.sum(far_weight[..., None] * picked, axis=2)
    ) / denominator[..., None]
    heads_out = (
        jnp.transpose(combined, (1, 0, 2, 3))
        .astype(jnp.bfloat16)
        .reshape(rows_local, query_heads * head_dim)
    )
    return lax.all_to_all(heads_out, "kvh", split_axis=0, concat_axis=1, tiled=True)


def solution(mesh):
    placed = (
        P("seq", "kvh", None),
        P(None, "seq", "kvh", None),
        P(None, "seq", None, "kvh", None),
        P("kvh", "seq", None),
        P(),
    )
    return jax.shard_map(
        per_device, mesh=mesh, in_specs=placed, out_specs=P(("seq", "kvh"), None), check_vma=False
    )
```

```python
import functools
import math

import jax
import jax.numpy as jnp
from jax import lax
from jax.experimental import pallas as pl
from jax.sharding import PartitionSpec as P

BLOCK_TOKENS = 2048
BLOCK_PICK_LIMIT = 2
WINDOW_SHIFTS = (8, 4, 16, 2, 1)
LOG2_E = 1.4426950408889634
SERVE_SPLIT = ((0, 2), (2, 3), (3, 4), (4, 5), (5, 8))


def shifted(value, axis, steps):
    count = lax.axis_size(axis)
    initial, last = (max(0, -steps), min(count, count - steps))
    return lax.ppermute(value, axis, [(source, source + steps) for source in range(initial, last)])


def gather_window(stretch_kv, span_devices, partner, companions):
    stack = stretch_kv[None]
    offsets = [0]
    results = []
    for index, step in enumerate(WINDOW_SHIFTS):
        if len(offsets) >= span_devices:
            break
        arrived = shifted(stack, "seq", step)
        if index < len(companions) and companions[index] is not None:
            arrived, done, partner = lax.optimization_barrier(
                (arrived, companions[index](partner), partner)
            )
            results.extend(done)
        stack = jnp.concatenate([stack, arrived], axis=0)
        offsets = offsets + [o + step for o in offsets]
    return stack, offsets, results


def attend_kernel(masked, scaling, group_size, *refs):
    if masked:
        thr_ref, q_ref, k_ref, v_ref, o_ref, lse_ref = refs
    else:
        q_ref, k_ref, v_ref, o_ref, lse_ref = refs
    q = q_ref[...]
    q = q.reshape(-1, q.shape[-1])
    scores = lax.dot_general(
        q, k_ref[...], (((1,), (1,)), ((), ())), preferred_element_type=jnp.float32
    )
    if masked:
        token = lax.broadcasted_iota(jnp.int32, (scores.shape[0], 1), 0) // group_size
        scores = jnp.where(token >= thr_ref[...], scores, -jnp.inf)
    highest = jnp.max(scores, axis=1, keepdims=True)
    raw_weights = jnp.exp2((scores - highest) * (scaling * LOG2_E))
    weight_sum = jnp.sum(raw_weights, axis=1, keepdims=True)
    blended = (
        jnp.dot(raw_weights.astype(jnp.bfloat16), v_ref[...], preferred_element_type=jnp.float32)
        / weight_sum
    )
    o_ref[...] = blended.astype(o_ref.dtype).reshape(o_ref.shape)
    log_sum = highest * scaling + jnp.log(weight_sum)
    lse_ref[...] = jnp.transpose(jnp.broadcast_to(log_sum, (log_sum.shape[0], 128)))[:8]


def attend(q, q_block, q_map, heads, tiles, keys, values, out_dtype, scaling, group_size, thr=None, out_rows=None, out_map=None):
    rows = q_block[0] * q_block[-2] if len(q_block) == 4 else q_block[-2]
    total_rows = rows * tiles
    key_count, head_dim = keys.shape[1], keys.shape[2]
    kv_spec = pl.BlockSpec((None, key_count, head_dim), lambda h, i: (h, 0, 0))
    in_specs = [pl.BlockSpec(q_block, q_map), kv_spec, kv_spec]
    operands = [q, keys, values]
    if thr is not None:
        in_specs = [pl.BlockSpec((1, key_count), lambda h, i: (0, 0))] + in_specs
        operands = [thr] + operands
    cost = pl.CostEstimate(
        flops=4 * heads * total_rows * key_count * head_dim,
        transcendentals=heads * total_rows * key_count,
        bytes_accessed=2 * (2 * heads * total_rows * head_dim + 2 * heads * key_count * head_dim),
    )
    return pl.pallas_call(
        functools.partial(attend_kernel, thr is not None, scaling, group_size),
        grid=(heads, tiles),
        in_specs=in_specs,
        out_specs=[
            pl.BlockSpec(q_block, out_map or q_map),
            pl.BlockSpec((None, None, 8, rows), lambda h, i: (h, i, 0, 0)),
        ],
        out_shape=[
            jax.ShapeDtypeStruct(((out_rows or q.shape[0]),) + q.shape[1:], out_dtype),
            jax.ShapeDtypeStruct((heads, tiles, 8, rows), jnp.float32),
        ],
        cost_estimate=cost,
    )(*operands)


def per_device(queries, stretch_kv, cache_kv, selection, block_owner):
    rows_local, query_heads, head_dim = queries.shape
    kv_heads = stretch_kv.shape[2]
    group_size = query_heads // kv_heads
    top_count = selection.shape[2]
    scaling = 1.0 / math.sqrt(head_dim)
    seq_count = lax.axis_size("seq")
    capacity = BLOCK_PICK_LIMIT
    span_devices = min(BLOCK_TOKENS // rows_local, seq_count)
    seq_place = lax.axis_index("seq")
    grouped = queries.reshape(rows_local, kv_heads, group_size, head_dim)
    requests = rows_local * top_count
    targets = block_owner[selection].reshape(kv_heads, requests)
    matches = (targets[:, :, None] == jnp.arange(seq_count, dtype=jnp.int32)[None, None, :]).astype(
        jnp.int32
    )
    places = jnp.sum((jnp.cumsum(matches, axis=1) - 1) * matches, axis=2)
    slots = targets * capacity + places
    one_hot = (
        (slots[:, None, :] == jnp.arange(seq_count * capacity, dtype=jnp.int32)[None, :, None])
        .astype(jnp.bfloat16)
        .reshape(kv_heads, seq_count, capacity, requests)
    )
    requested = jnp.repeat(jnp.swapaxes(grouped, 0, 1), top_count, axis=1).reshape(
        kv_heads, requests, group_size * head_dim
    )
    outgoing = jnp.einsum(
        "htcr,hrx->thcx", one_hot, requested, preferred_element_type=jnp.float32
    ).astype(jnp.bfloat16)
    slab = capacity * group_size
    outgoing = outgoing.reshape(seq_count, kv_heads, slab, head_dim)
    arrived = lax.all_to_all(outgoing, "seq", split_axis=0, concat_axis=0, tiled=True)
    arrived, window_start = lax.optimization_barrier((arrived, stretch_kv))
    cache_keys = jnp.swapaxes(cache_kv[0, 0], 0, 1)
    cache_values = jnp.swapaxes(cache_kv[1, 0], 0, 1)
    sources_per_tile = 16
    pieces = seq_count // sources_per_tile

    def serve_piece(piece, arrived):
        return attend(
            arrived[piece * sources_per_tile : (piece + 1) * sources_per_tile],
            (sources_per_tile, None, slab, head_dim),
            lambda h, i: (0, h, 0, 0),
            kv_heads,
            1,
            cache_keys,
            cache_values,
            jnp.bfloat16,
            scaling,
            group_size,
        )

    def serve_pieces(first, last, arrived):
        return tuple(serve_piece(piece, arrived) for piece in range(first, last))

    window, offsets, served_pieces = gather_window(
        window_start,
        span_devices,
        arrived,
        [functools.partial(serve_pieces, first, last) for first, last in SERVE_SPLIT],
    )
    blocks = window.shape[0]
    served = jnp.concatenate([piece[0] for piece in served_pieces], axis=0)
    served_lse = jnp.concatenate(
        [piece[1][:, :, 0].reshape(kv_heads, sources_per_tile, slab) for piece in served_pieces], axis=1
    )
    served_lse = jnp.swapaxes(served_lse, 0, 1)
    served, served_lse, window = lax.optimization_barrier((served, served_lse, window))
    lse_rounded = lax.reduce_precision(served_lse, exponent_bits=8, mantissa_bits=7)
    lse_high = lse_rounded.astype(jnp.bfloat16)
    lse_low = (served_lse - lse_rounded).astype(jnp.bfloat16)
    payload_width = kv_heads * slab * head_dim
    lse_width = 2 * kv_heads * slab
    lse_lanes = -(-lse_width // 128) * 128
    lse_pack = jnp.concatenate([lse_high, lse_low], axis=2).reshape(seq_count, lse_width)
    payload = jnp.concatenate(
        [
            served.reshape(seq_count, payload_width),
            jnp.pad(lse_pack, ((0, 0), (0, lse_lanes - lse_width))),
        ],
        axis=1,
    )
    returned = lax.all_to_all(payload, "seq", split_axis=0, concat_axis=0, tiled=True)
    answers = returned[:, :payload_width].reshape(seq_count, kv_heads, capacity, group_size * head_dim)
    lse_parts = returned[:, payload_width : payload_width + lse_width].reshape(
        seq_count, kv_heads, 2, capacity, group_size
    )
    lse_parts = jnp.swapaxes(lse_parts, 2, 3).reshape(seq_count, kv_heads, capacity, 2 * group_size)
    window_keys = jnp.transpose(window[:, 0], (2, 0, 1, 3)).reshape(kv_heads, blocks * rows_local, head_dim)
    window_values = jnp.transpose(window[:, 1], (2, 0, 1, 3)).reshape(kv_heads, blocks * rows_local, head_dim)
    key_index = jnp.arange(blocks * rows_local, dtype=jnp.int32)
    key_offset = jnp.asarray(offsets, jnp.int32)[key_index // rows_local]
    threshold = jnp.where(
        seq_place - key_offset >= 0,
        jnp.where(key_offset == 0, key_index % rows_local, 0),
        rows_local,
    )[None, :]
    window_queries = jnp.swapaxes(grouped, 0, 1).reshape(kv_heads, rows_local * group_size, head_dim)
    own_out, own_lse = attend(
        window_queries,
        (None, rows_local * group_size, head_dim),
        lambda h, i: (h, 0, 0),
        kv_heads,
        1,
        window_keys,
        window_values,
        jnp.float32,
        scaling,
        group_size,
        threshold,
    )
    own_out = own_out.reshape(kv_heads, rows_local, group_size, head_dim)
    own_lse = own_lse[:, :, 0].reshape(kv_heads, rows_local, group_size)
    head_rows = jnp.arange(kv_heads, dtype=jnp.int32)[:, None]
    picked = (
        jnp.einsum(
            "htcr,thcx->hrx",
            one_hot,
            answers,
            preferred_element_type=jnp.float32,
        )
        .reshape(kv_heads, rows_local, top_count, group_size, head_dim)
    )
    picked_parts = jnp.einsum(
        "htcr,thcx->hrx", one_hot, lse_parts, preferred_element_type=jnp.float32
    )
    picked_lse = (picked_parts[..., :group_size] + picked_parts[..., group_size:]).reshape(
        kv_heads, rows_local, top_count, group_size
    )
    ceiling = jnp.maximum(own_lse, jnp.max(picked_lse, axis=2))
    own_weight = jnp.exp(own_lse - ceiling)
    far_weight = jnp.exp(picked_lse - ceiling[:, :, None])
    denominator = own_weight + jnp.sum(far_weight, axis=2)
    combined = (
        own_weight[..., None] * own_out + jnp.sum(far_weight[..., None] * picked, axis=2)
    ) / denominator[..., None]
    heads_out = (
        jnp.transpose(combined, (1, 0, 2, 3))
        .astype(jnp.bfloat16)
        .reshape(rows_local, query_heads * head_dim)
    )
    return lax.all_to_all(heads_out, "kvh", split_axis=0, concat_axis=1, tiled=True)


def solution(mesh):
    placed = (
        P("seq", "kvh", None),
        P(None, "seq", "kvh", None),
        P(None, "seq", None, "kvh", None),
        P("kvh", "seq", None),
        P(),
    )
    return jax.shard_map(
        per_device, mesh=mesh, in_specs=placed, out_specs=P(("seq", "kvh"), None), check_vma=False
    )
```

```python
import functools
import math

import jax
import jax.numpy as jnp
from jax import lax
from jax.experimental import pallas as pl
from jax.sharding import PartitionSpec as P

BLOCK_TOKENS = 2048
BLOCK_PICK_LIMIT = 2
WINDOW_SHIFTS = (8, 4, 16, 2, 1)
LOG2_E = 1.4426950408889634


def shifted(value, axis, steps):
    count = lax.axis_size(axis)
    initial, last = (max(0, -steps), min(count, count - steps))
    return lax.ppermute(value, axis, [(source, source + steps) for source in range(initial, last)])


def gather_window(stretch_kv, span_devices, companions):
    stack = stretch_kv[None]
    offsets = [0]
    results = []
    for index, step in enumerate(WINDOW_SHIFTS):
        if len(offsets) >= span_devices:
            break
        arrived = shifted(stack, "seq", step)
        if index < len(companions) and companions[index] is not None:
            arrived, done = lax.optimization_barrier((arrived, companions[index]()))
            results.append(done)
        stack = jnp.concatenate([stack, arrived], axis=0)
        offsets = offsets + [o + step for o in offsets]
    return stack, offsets, results


def attend_kernel(masked, scaling, group_size, *refs):
    if masked:
        thr_ref, q_ref, k_ref, v_ref, o_ref, lse_ref = refs
    else:
        q_ref, k_ref, v_ref, o_ref, lse_ref = refs
    q = q_ref[...]
    q = q.reshape(-1, q.shape[-1])
    scores = lax.dot_general(
        q, k_ref[...], (((1,), (1,)), ((), ())), preferred_element_type=jnp.float32
    )
    if masked:
        token = lax.broadcasted_iota(jnp.int32, (scores.shape[0], 1), 0) // group_size
        scores = jnp.where(token >= thr_ref[...], scores, -jnp.inf)
    highest = jnp.max(scores, axis=1, keepdims=True)
    raw_weights = jnp.exp2((scores - highest) * (scaling * LOG2_E))
    weight_sum = jnp.sum(raw_weights, axis=1, keepdims=True)
    blended = (
        jnp.dot(raw_weights.astype(jnp.bfloat16), v_ref[...], preferred_element_type=jnp.float32)
        / weight_sum
    )
    o_ref[...] = blended.astype(o_ref.dtype).reshape(o_ref.shape)
    log_sum = highest * scaling + jnp.log(weight_sum)
    lse_ref[...] = jnp.transpose(jnp.broadcast_to(log_sum, (log_sum.shape[0], 128)))[:8]


def attend(q, q_block, q_map, heads, tiles, keys, values, out_dtype, scaling, group_size, thr=None, out_rows=None, out_map=None):
    rows = q_block[0] * q_block[-2] if len(q_block) == 4 else q_block[-2]
    total_rows = rows * tiles
    key_count, head_dim = keys.shape[1], keys.shape[2]
    kv_spec = pl.BlockSpec((None, key_count, head_dim), lambda h, i: (h, 0, 0))
    in_specs = [pl.BlockSpec(q_block, q_map), kv_spec, kv_spec]
    operands = [q, keys, values]
    if thr is not None:
        in_specs = [pl.BlockSpec((1, key_count), lambda h, i: (0, 0))] + in_specs
        operands = [thr] + operands
    cost = pl.CostEstimate(
        flops=4 * heads * total_rows * key_count * head_dim,
        transcendentals=heads * total_rows * key_count,
        bytes_accessed=2 * (2 * heads * total_rows * head_dim + 2 * heads * key_count * head_dim),
    )
    return pl.pallas_call(
        functools.partial(attend_kernel, thr is not None, scaling, group_size),
        grid=(heads, tiles),
        in_specs=in_specs,
        out_specs=[
            pl.BlockSpec(q_block, out_map or q_map),
            pl.BlockSpec((None, None, 8, rows), lambda h, i: (h, i, 0, 0)),
        ],
        out_shape=[
            jax.ShapeDtypeStruct(((out_rows or q.shape[0]),) + q.shape[1:], out_dtype),
            jax.ShapeDtypeStruct((heads, tiles, 8, rows), jnp.float32),
        ],
        cost_estimate=cost,
    )(*operands)


def per_device(queries, stretch_kv, cache_kv, selection, block_owner):
    rows_local, query_heads, head_dim = queries.shape
    kv_heads = stretch_kv.shape[2]
    group_size = query_heads // kv_heads
    top_count = selection.shape[2]
    scaling = 1.0 / math.sqrt(head_dim)
    seq_count = lax.axis_size("seq")
    capacity = BLOCK_PICK_LIMIT
    span_devices = min(BLOCK_TOKENS // rows_local, seq_count)
    seq_place = lax.axis_index("seq")
    grouped = queries.reshape(rows_local, kv_heads, group_size, head_dim)
    requests = rows_local * top_count
    owners = jnp.arange(block_owner.shape[0], dtype=jnp.int32)
    targets = jnp.sum(
        jnp.where(selection[..., None] == owners, block_owner, 0), axis=-1
    ).reshape(kv_heads, requests)
    matches = (targets[:, :, None] == jnp.arange(seq_count, dtype=jnp.int32)[None, None, :]).astype(
        jnp.int32
    )
    places = jnp.sum((jnp.cumsum(matches, axis=1) - 1) * matches, axis=2)
    slots = targets * capacity + places
    one_hot = (
        (slots[:, None, :] == jnp.arange(seq_count * capacity, dtype=jnp.int32)[None, :, None])
        .astype(jnp.bfloat16)
        .reshape(kv_heads, seq_count, capacity, requests)
    )
    requested = jnp.repeat(jnp.swapaxes(grouped, 0, 1), top_count, axis=1)
    outgoing = jnp.einsum(
        "htcr,hrgd->thcgd", one_hot, requested, preferred_element_type=jnp.float32
    ).astype(jnp.bfloat16)
    slab = capacity * group_size
    outgoing = outgoing.reshape(seq_count, kv_heads, slab, head_dim)
    arrived = lax.all_to_all(outgoing, "seq", split_axis=0, concat_axis=0, tiled=True)
    arrived, window_start = lax.optimization_barrier((arrived, stretch_kv))
    cache_keys = jnp.swapaxes(cache_kv[0, 0], 0, 1)
    cache_values = jnp.swapaxes(cache_kv[1, 0], 0, 1)
    sources_per_tile = 32
    pieces = seq_count // sources_per_tile

    def serve_piece(piece):
        return attend(
            arrived[piece * sources_per_tile : (piece + 1) * sources_per_tile],
            (sources_per_tile, None, slab, head_dim),
            lambda h, i: (0, h, 0, 0),
            kv_heads,
            1,
            cache_keys,
            cache_values,
            jnp.bfloat16,
            scaling,
            group_size,
        )

    window, offsets, served_pieces = gather_window(
        window_start,
        span_devices,
        [None] + [functools.partial(serve_piece, piece) for piece in range(pieces)],
    )
    blocks = window.shape[0]
    served = jnp.concatenate([piece[0] for piece in served_pieces], axis=0)
    served_lse = jnp.concatenate(
        [piece[1][:, :, 0].reshape(kv_heads, sources_per_tile, slab) for piece in served_pieces], axis=1
    )
    served_lse = jnp.swapaxes(served_lse, 0, 1)
    served, served_lse, window = lax.optimization_barrier((served, served_lse, window))
    lse_rounded = lax.reduce_precision(served_lse, exponent_bits=8, mantissa_bits=7)
    lse_high = lse_rounded.astype(jnp.bfloat16)
    lse_low = (served_lse - lse_rounded).astype(jnp.bfloat16)
    payload_width = kv_heads * slab * head_dim
    lse_width = 2 * kv_heads * slab
    lse_lanes = -(-lse_width // 128) * 128
    lse_pack = jnp.concatenate([lse_high, lse_low], axis=2).reshape(seq_count, lse_width)
    payload = jnp.concatenate(
        [
            served.reshape(seq_count, payload_width),
            jnp.pad(lse_pack, ((0, 0), (0, lse_lanes - lse_width))),
        ],
        axis=1,
    )
    returned = lax.all_to_all(payload, "seq", split_axis=0, concat_axis=0, tiled=True)
    answers = returned[:, :payload_width].reshape(seq_count, kv_heads, capacity, group_size * head_dim)
    lse_parts = returned[:, payload_width : payload_width + lse_width].reshape(
        seq_count, kv_heads, 2, capacity, group_size
    )
    lse_parts = jnp.swapaxes(lse_parts, 2, 3).reshape(seq_count, kv_heads, capacity, 2 * group_size)
    window_keys = jnp.transpose(window[:, 0], (2, 0, 1, 3)).reshape(kv_heads, blocks * rows_local, head_dim)
    window_values = jnp.transpose(window[:, 1], (2, 0, 1, 3)).reshape(kv_heads, blocks * rows_local, head_dim)
    key_index = jnp.arange(blocks * rows_local, dtype=jnp.int32)
    key_offset = jnp.asarray(offsets, jnp.int32)[key_index // rows_local]
    threshold = jnp.where(
        seq_place - key_offset >= 0,
        jnp.where(key_offset == 0, key_index % rows_local, 0),
        rows_local,
    )[None, :]
    window_queries = jnp.swapaxes(grouped, 0, 1).reshape(kv_heads, rows_local * group_size, head_dim)
    own_out, own_lse = attend(
        window_queries,
        (None, rows_local * group_size, head_dim),
        lambda h, i: (h, 0, 0),
        kv_heads,
        1,
        window_keys,
        window_values,
        jnp.float32,
        scaling,
        group_size,
        threshold,
    )
    own_out = own_out.reshape(kv_heads, rows_local, group_size, head_dim)
    own_lse = own_lse[:, :, 0].reshape(kv_heads, rows_local, group_size)
    head_rows = jnp.arange(kv_heads, dtype=jnp.int32)[:, None]
    picked = (
        jnp.einsum(
            "htcr,thcx->hrx",
            one_hot,
            answers,
            preferred_element_type=jnp.float32,
        )
        .reshape(kv_heads, rows_local, top_count, group_size, head_dim)
    )
    picked_parts = jnp.einsum(
        "htcr,thcx->hrx", one_hot, lse_parts, preferred_element_type=jnp.float32
    )
    picked_lse = (picked_parts[..., :group_size] + picked_parts[..., group_size:]).reshape(
        kv_heads, rows_local, top_count, group_size
    )
    ceiling = jnp.maximum(own_lse, jnp.max(picked_lse, axis=2))
    own_weight = jnp.exp(own_lse - ceiling)
    far_weight = jnp.exp(picked_lse - ceiling[:, :, None])
    denominator = own_weight + jnp.sum(far_weight, axis=2)
    combined = (
        own_weight[..., None] * own_out + jnp.sum(far_weight[..., None] * picked, axis=2)
    ) / denominator[..., None]
    heads_out = (
        jnp.transpose(combined, (1, 0, 2, 3))
        .astype(jnp.bfloat16)
        .reshape(rows_local, query_heads * head_dim)
    )
    return lax.all_to_all(heads_out, "kvh", split_axis=0, concat_axis=1, tiled=True)


def solution(mesh):
    placed = (
        P("seq", "kvh", None),
        P(None, "seq", "kvh", None),
        P(None, "seq", None, "kvh", None),
        P("kvh", "seq", None),
        P(),
    )
    return jax.shard_map(
        per_device, mesh=mesh, in_specs=placed, out_specs=P(("seq", "kvh"), None), check_vma=False
    )
```

```python
import functools
import math

import jax
import jax.numpy as jnp
from jax import lax
from jax.experimental import pallas as pl
from jax.sharding import PartitionSpec as P

BLOCK_TOKENS = 2048
BLOCK_PICK_LIMIT = 2
WINDOW_SHIFTS = (16, 8, 4, 2, 1)
LOG2_E = 1.4426950408889634


def shifted(value, axis, steps):
    count = lax.axis_size(axis)
    initial, last = (max(0, -steps), min(count, count - steps))
    return lax.ppermute(value, axis, [(source, source + steps) for source in range(initial, last)])


def gather_window(stretch_kv, span_devices, companions):
    stack = stretch_kv[None]
    offsets = [0]
    results = []
    for index, step in enumerate(WINDOW_SHIFTS):
        if len(offsets) >= span_devices:
            break
        arrived = shifted(stack, "seq", step)
        if index < len(companions) and companions[index] is not None:
            arrived, done = lax.optimization_barrier((arrived, companions[index]()))
            results.append(done)
        stack = jnp.concatenate([stack, arrived], axis=0)
        offsets = offsets + [o + step for o in offsets]
    return stack, offsets, results


def attend_kernel(masked, scaling, group_size, *refs):
    if masked:
        thr_ref, q_ref, k_ref, v_ref, o_ref, lse_ref = refs
    else:
        q_ref, k_ref, v_ref, o_ref, lse_ref = refs
    q = q_ref[...]
    q = q.reshape(-1, q.shape[-1])
    scores = lax.dot_general(
        q, k_ref[...], (((1,), (1,)), ((), ())), preferred_element_type=jnp.float32
    )
    if masked:
        token = lax.broadcasted_iota(jnp.int32, (scores.shape[0], 1), 0) // group_size
        scores = jnp.where(token >= thr_ref[...], scores, -jnp.inf)
    highest = jnp.max(scores, axis=1, keepdims=True)
    raw_weights = jnp.exp2((scores - highest) * (scaling * LOG2_E))
    weight_sum = jnp.sum(raw_weights, axis=1, keepdims=True)
    blended = (
        jnp.dot(raw_weights.astype(jnp.bfloat16), v_ref[...], preferred_element_type=jnp.float32)
        / weight_sum
    )
    o_ref[...] = blended.astype(o_ref.dtype).reshape(o_ref.shape)
    log_sum = highest * scaling + jnp.log(weight_sum)
    lse_ref[...] = jnp.transpose(jnp.broadcast_to(log_sum, (log_sum.shape[0], 128)))[:8]


def attend(q, q_block, q_map, heads, tiles, keys, values, out_dtype, scaling, group_size, thr=None, out_rows=None, out_map=None):
    rows = q_block[0] * q_block[-2] if len(q_block) == 4 else q_block[-2]
    total_rows = rows * tiles
    key_count, head_dim = keys.shape[1], keys.shape[2]
    kv_spec = pl.BlockSpec((None, key_count, head_dim), lambda h, i: (h, 0, 0))
    in_specs = [pl.BlockSpec(q_block, q_map), kv_spec, kv_spec]
    operands = [q, keys, values]
    if thr is not None:
        in_specs = [pl.BlockSpec((1, key_count), lambda h, i: (0, 0))] + in_specs
        operands = [thr] + operands
    cost = pl.CostEstimate(
        flops=4 * heads * total_rows * key_count * head_dim,
        transcendentals=heads * total_rows * key_count,
        bytes_accessed=2 * (2 * heads * total_rows * head_dim + 2 * heads * key_count * head_dim),
    )
    return pl.pallas_call(
        functools.partial(attend_kernel, thr is not None, scaling, group_size),
        grid=(heads, tiles),
        in_specs=in_specs,
        out_specs=[
            pl.BlockSpec(q_block, out_map or q_map),
            pl.BlockSpec((None, None, 8, rows), lambda h, i: (h, i, 0, 0)),
        ],
        out_shape=[
            jax.ShapeDtypeStruct(((out_rows or q.shape[0]),) + q.shape[1:], out_dtype),
            jax.ShapeDtypeStruct((heads, tiles, 8, rows), jnp.float32),
        ],
        cost_estimate=cost,
    )(*operands)


def per_device(queries, stretch_kv, cache_kv, selection, block_owner):
    rows_local, query_heads, head_dim = queries.shape
    kv_heads = stretch_kv.shape[2]
    group_size = query_heads // kv_heads
    top_count = selection.shape[2]
    scaling = 1.0 / math.sqrt(head_dim)
    seq_count = lax.axis_size("seq")
    capacity = BLOCK_PICK_LIMIT
    span_devices = min(BLOCK_TOKENS // rows_local, seq_count)
    seq_place = lax.axis_index("seq")
    grouped = queries.reshape(rows_local, kv_heads, group_size, head_dim)
    requests = rows_local * top_count
    owners = jnp.arange(block_owner.shape[0], dtype=jnp.int32)
    targets = jnp.sum(
        jnp.where(selection[..., None] == owners, block_owner, 0), axis=-1
    ).reshape(kv_heads, requests)
    matches = (targets[:, :, None] == jnp.arange(seq_count, dtype=jnp.int32)[None, None, :]).astype(
        jnp.int32
    )
    places = jnp.sum((jnp.cumsum(matches, axis=1) - 1) * matches, axis=2)
    slots = targets * capacity + places
    one_hot = (
        (slots[:, None, :] == jnp.arange(seq_count * capacity, dtype=jnp.int32)[None, :, None])
        .astype(jnp.bfloat16)
        .reshape(kv_heads, seq_count, capacity, requests)
    )
    requested = jnp.repeat(jnp.swapaxes(grouped, 0, 1), top_count, axis=1)
    outgoing = jnp.einsum(
        "htcr,hrgd->thcgd", one_hot, requested, preferred_element_type=jnp.float32
    ).astype(jnp.bfloat16)
    slab = capacity * group_size
    outgoing = outgoing.reshape(seq_count, kv_heads, slab, head_dim)
    arrived = lax.all_to_all(outgoing, "seq", split_axis=0, concat_axis=0, tiled=True)
    arrived, window_start = lax.optimization_barrier((arrived, stretch_kv))
    cache_keys = jnp.swapaxes(cache_kv[0, 0], 0, 1)
    cache_values = jnp.swapaxes(cache_kv[1, 0], 0, 1)
    sources_per_tile = 32
    pieces = seq_count // sources_per_tile

    def serve_piece(piece):
        return attend(
            arrived[piece * sources_per_tile : (piece + 1) * sources_per_tile],
            (sources_per_tile, None, slab, head_dim),
            lambda h, i: (0, h, 0, 0),
            kv_heads,
            1,
            cache_keys,
            cache_values,
            jnp.bfloat16,
            scaling,
            group_size,
        )

    window, offsets, served_pieces = gather_window(
        window_start,
        span_devices,
        [None] + [functools.partial(serve_piece, piece) for piece in range(pieces)],
    )
    blocks = window.shape[0]
    served = jnp.concatenate([piece[0] for piece in served_pieces], axis=0)
    served_lse = jnp.concatenate(
        [piece[1][:, :, 0].reshape(kv_heads, sources_per_tile, slab) for piece in served_pieces], axis=1
    )
    served_lse = jnp.swapaxes(served_lse, 0, 1)
    served, served_lse, window = lax.optimization_barrier((served, served_lse, window))
    lse_rounded = lax.reduce_precision(served_lse, exponent_bits=8, mantissa_bits=7)
    lse_high = lse_rounded.astype(jnp.bfloat16)
    lse_low = (served_lse - lse_rounded).astype(jnp.bfloat16)
    payload_width = kv_heads * slab * head_dim
    lse_width = 2 * kv_heads * slab
    lse_lanes = -(-lse_width // 128) * 128
    lse_pack = jnp.concatenate([lse_high, lse_low], axis=2).reshape(seq_count, lse_width)
    payload = jnp.concatenate(
        [
            served.reshape(seq_count, payload_width),
            jnp.pad(lse_pack, ((0, 0), (0, lse_lanes - lse_width))),
        ],
        axis=1,
    )
    returned = lax.all_to_all(payload, "seq", split_axis=0, concat_axis=0, tiled=True)
    answers = returned[:, :payload_width].reshape(seq_count, kv_heads, capacity, group_size * head_dim)
    lse_parts = returned[:, payload_width : payload_width + lse_width].reshape(
        seq_count, kv_heads, 2, capacity, group_size
    )
    lse_parts = jnp.swapaxes(lse_parts, 2, 3).reshape(seq_count, kv_heads, capacity, 2 * group_size)
    window_keys = jnp.transpose(window[:, 0], (2, 0, 1, 3)).reshape(kv_heads, blocks * rows_local, head_dim)
    window_values = jnp.transpose(window[:, 1], (2, 0, 1, 3)).reshape(kv_heads, blocks * rows_local, head_dim)
    key_index = jnp.arange(blocks * rows_local, dtype=jnp.int32)
    key_offset = jnp.asarray(offsets, jnp.int32)[key_index // rows_local]
    threshold = jnp.where(
        seq_place - key_offset >= 0,
        jnp.where(key_offset == 0, key_index % rows_local, 0),
        rows_local,
    )[None, :]
    window_queries = jnp.swapaxes(grouped, 0, 1).reshape(kv_heads, rows_local * group_size, head_dim)
    own_out, own_lse = attend(
        window_queries,
        (None, rows_local * group_size, head_dim),
        lambda h, i: (h, 0, 0),
        kv_heads,
        1,
        window_keys,
        window_values,
        jnp.float32,
        scaling,
        group_size,
        threshold,
    )
    own_out = own_out.reshape(kv_heads, rows_local, group_size, head_dim)
    own_lse = own_lse[:, :, 0].reshape(kv_heads, rows_local, group_size)
    head_rows = jnp.arange(kv_heads, dtype=jnp.int32)[:, None]
    picked = (
        jnp.einsum(
            "htcr,thcx->hrx",
            one_hot,
            answers,
            preferred_element_type=jnp.float32,
        )
        .reshape(kv_heads, rows_local, top_count, group_size, head_dim)
    )
    picked_parts = jnp.einsum(
        "htcr,thcx->hrx", one_hot, lse_parts, preferred_element_type=jnp.float32
    )
    picked_lse = (picked_parts[..., :group_size] + picked_parts[..., group_size:]).reshape(
        kv_heads, rows_local, top_count, group_size
    )
    ceiling = jnp.maximum(own_lse, jnp.max(picked_lse, axis=2))
    own_weight = jnp.exp(own_lse - ceiling)
    far_weight = jnp.exp(picked_lse - ceiling[:, :, None])
    denominator = own_weight + jnp.sum(far_weight, axis=2)
    combined = (
        own_weight[..., None] * own_out + jnp.sum(far_weight[..., None] * picked, axis=2)
    ) / denominator[..., None]
    heads_out = (
        jnp.transpose(combined, (1, 0, 2, 3))
        .astype(jnp.bfloat16)
        .reshape(rows_local, query_heads * head_dim)
    )
    return lax.all_to_all(heads_out, "kvh", split_axis=0, concat_axis=1, tiled=True)


def solution(mesh):
    placed = (
        P("seq", "kvh", None),
        P(None, "seq", "kvh", None),
        P(None, "seq", None, "kvh", None),
        P("kvh", "seq", None),
        P(),
    )
    return jax.shard_map(
        per_device, mesh=mesh, in_specs=placed, out_specs=P(("seq", "kvh"), None), check_vma=False
    )
```

```python
import functools
import math

import jax
import jax.numpy as jnp
from jax import lax
from jax.experimental import pallas as pl
from jax.sharding import PartitionSpec as P

BLOCK_TOKENS = 2048
BLOCK_PICK_LIMIT = 2
WINDOW_SHIFTS = (8, 4, 16, 2, 1)
LOG2_E = 1.4426950408889634


def shifted(value, axis, steps):
    count = lax.axis_size(axis)
    initial, last = (max(0, -steps), min(count, count - steps))
    return lax.ppermute(value, axis, [(source, source + steps) for source in range(initial, last)])


def gather_window(stretch_kv, span_devices, companions):
    stack = stretch_kv[None]
    offsets = [0]
    results = []
    for index, step in enumerate(WINDOW_SHIFTS):
        if len(offsets) >= span_devices:
            break
        arrived = shifted(stack, "seq", step)
        if index < len(companions) and companions[index] is not None:
            arrived, done = lax.optimization_barrier((arrived, companions[index]()))
            results.append(done)
        stack = jnp.concatenate([stack, arrived], axis=0)
        offsets = offsets + [o + step for o in offsets]
    return stack, offsets, results


def attend_kernel(masked, scaling, group_size, *refs):
    if masked:
        thr_ref, q_ref, k_ref, v_ref, o_ref, lse_ref = refs
    else:
        q_ref, k_ref, v_ref, o_ref, lse_ref = refs
    q = q_ref[...]
    q = q.reshape(-1, q.shape[-1])
    scores = lax.dot_general(
        q, k_ref[...], (((1,), (1,)), ((), ())), preferred_element_type=jnp.float32
    )
    if masked:
        token = lax.broadcasted_iota(jnp.int32, (scores.shape[0], 1), 0) // group_size
        scores = jnp.where(token >= thr_ref[...], scores, -jnp.inf)
    highest = jnp.max(scores, axis=1, keepdims=True)
    raw_weights = jnp.exp2((scores - highest) * (scaling * LOG2_E))
    weight_sum = jnp.sum(raw_weights, axis=1, keepdims=True)
    blended = (
        jnp.dot(raw_weights.astype(jnp.bfloat16), v_ref[...], preferred_element_type=jnp.float32)
        / weight_sum
    )
    o_ref[...] = blended.astype(o_ref.dtype).reshape(o_ref.shape)
    log_sum = highest * scaling + jnp.log(weight_sum)
    lse_ref[...] = jnp.transpose(jnp.broadcast_to(log_sum, (log_sum.shape[0], 128)))[:8]


def attend(q, q_block, q_map, heads, tiles, keys, values, out_dtype, scaling, group_size, thr=None, out_rows=None, out_map=None):
    rows = q_block[0] * q_block[-2] if len(q_block) == 4 else q_block[-2]
    total_rows = rows * tiles
    key_count, head_dim = keys.shape[1], keys.shape[2]
    kv_spec = pl.BlockSpec((None, key_count, head_dim), lambda h, i: (h, 0, 0))
    in_specs = [pl.BlockSpec(q_block, q_map), kv_spec, kv_spec]
    operands = [q, keys, values]
    if thr is not None:
        in_specs = [pl.BlockSpec((1, key_count), lambda h, i: (0, 0))] + in_specs
        operands = [thr] + operands
    cost = pl.CostEstimate(
        flops=4 * heads * total_rows * key_count * head_dim,
        transcendentals=heads * total_rows * key_count,
        bytes_accessed=2 * (2 * heads * total_rows * head_dim + 2 * heads * key_count * head_dim),
    )
    return pl.pallas_call(
        functools.partial(attend_kernel, thr is not None, scaling, group_size),
        grid=(heads, tiles),
        in_specs=in_specs,
        out_specs=[
            pl.BlockSpec(q_block, out_map or q_map),
            pl.BlockSpec((None, None, 8, rows), lambda h, i: (h, i, 0, 0)),
        ],
        out_shape=[
            jax.ShapeDtypeStruct(((out_rows or q.shape[0]),) + q.shape[1:], out_dtype),
            jax.ShapeDtypeStruct((heads, tiles, 8, rows), jnp.float32),
        ],
        cost_estimate=cost,
    )(*operands)


def per_device(queries, stretch_kv, cache_kv, selection, block_owner):
    rows_local, query_heads, head_dim = queries.shape
    kv_heads = stretch_kv.shape[2]
    group_size = query_heads // kv_heads
    top_count = selection.shape[2]
    scaling = 1.0 / math.sqrt(head_dim)
    seq_count = lax.axis_size("seq")
    capacity = BLOCK_PICK_LIMIT
    span_devices = min(BLOCK_TOKENS // rows_local, seq_count)
    seq_place = lax.axis_index("seq")
    grouped = queries.reshape(rows_local, kv_heads, group_size, head_dim)
    requests = rows_local * top_count
    owners = jnp.arange(block_owner.shape[0], dtype=jnp.int32)
    targets = jnp.sum(
        jnp.where(selection[..., None] == owners, block_owner, 0), axis=-1
    ).reshape(kv_heads, requests)
    matches = (targets[:, :, None] == jnp.arange(seq_count, dtype=jnp.int32)[None, None, :]).astype(
        jnp.int32
    )
    places = jnp.sum((jnp.cumsum(matches, axis=1) - 1) * matches, axis=2)
    slots = targets * capacity + places
    one_hot = (
        (slots[:, None, :] == jnp.arange(seq_count * capacity, dtype=jnp.int32)[None, :, None])
        .astype(jnp.bfloat16)
        .reshape(kv_heads, seq_count, capacity, requests)
    )
    requested = jnp.repeat(jnp.swapaxes(grouped, 0, 1), top_count, axis=1)
    outgoing = jnp.einsum(
        "htcr,hrgd->thcgd", one_hot, requested, preferred_element_type=jnp.float32
    ).astype(jnp.bfloat16)
    slab = capacity * group_size
    outgoing = outgoing.reshape(seq_count, kv_heads, slab, head_dim)
    arrived = lax.all_to_all(outgoing, "seq", split_axis=0, concat_axis=0, tiled=True)
    arrived, window_start = lax.optimization_barrier((arrived, stretch_kv))
    cache_keys = jnp.swapaxes(cache_kv[0, 0], 0, 1)
    cache_values = jnp.swapaxes(cache_kv[1, 0], 0, 1)
    sources_per_tile = 32
    pieces = seq_count // sources_per_tile

    def serve_piece(piece):
        return attend(
            arrived[piece * sources_per_tile : (piece + 1) * sources_per_tile],
            (sources_per_tile, None, slab, head_dim),
            lambda h, i: (0, h, 0, 0),
            kv_heads,
            1,
            cache_keys,
            cache_values,
            jnp.bfloat16,
            scaling,
            group_size,
        )

    window, offsets, served_pieces = gather_window(
        window_start,
        span_devices,
        [None] + [functools.partial(serve_piece, piece) for piece in range(pieces)],
    )
    blocks = window.shape[0]
    served = jnp.concatenate([piece[0] for piece in served_pieces], axis=0)
    served_lse = jnp.concatenate([piece[1] for piece in served_pieces], axis=1)[:, :, 0]
    served_lse = served_lse.reshape(kv_heads, seq_count, slab)
    served_lse = jnp.swapaxes(served_lse, 0, 1)
    served, served_lse, window = lax.optimization_barrier((served, served_lse, window))
    lse_rounded = lax.reduce_precision(served_lse, exponent_bits=8, mantissa_bits=7)
    lse_high = lse_rounded.astype(jnp.bfloat16)
    lse_low = (served_lse - lse_rounded).astype(jnp.bfloat16)
    payload_width = kv_heads * slab * head_dim
    lse_width = 2 * kv_heads * slab
    lse_lanes = -(-lse_width // 128) * 128
    lse_pack = jnp.concatenate([lse_high, lse_low], axis=2).reshape(seq_count, lse_width)
    payload = jnp.concatenate(
        [
            served.reshape(seq_count, payload_width),
            jnp.pad(lse_pack, ((0, 0), (0, lse_lanes - lse_width))),
        ],
        axis=1,
    )
    returned = lax.all_to_all(payload, "seq", split_axis=0, concat_axis=0, tiled=True)
    answers = returned[:, :payload_width].reshape(seq_count, kv_heads, capacity, group_size * head_dim)
    lse_parts = returned[:, payload_width : payload_width + lse_width].reshape(
        seq_count, kv_heads, 2, capacity, group_size
    )
    lse_parts = jnp.swapaxes(lse_parts, 2, 3).reshape(seq_count, kv_heads, capacity, 2 * group_size)
    window_keys = jnp.transpose(window[:, 0], (2, 0, 1, 3)).reshape(kv_heads, blocks * rows_local, head_dim)
    window_values = jnp.transpose(window[:, 1], (2, 0, 1, 3)).reshape(kv_heads, blocks * rows_local, head_dim)
    key_index = jnp.arange(blocks * rows_local, dtype=jnp.int32)
    key_offset = jnp.asarray(offsets, jnp.int32)[key_index // rows_local]
    threshold = jnp.where(
        seq_place - key_offset >= 0,
        jnp.where(key_offset == 0, key_index % rows_local, 0),
        rows_local,
    )[None, :]
    window_queries = jnp.swapaxes(grouped, 0, 1).reshape(kv_heads, rows_local * group_size, head_dim)
    own_out, own_lse = attend(
        window_queries,
        (None, rows_local * group_size, head_dim),
        lambda h, i: (h, 0, 0),
        kv_heads,
        1,
        window_keys,
        window_values,
        jnp.float32,
        scaling,
        group_size,
        threshold,
    )
    own_out = own_out.reshape(kv_heads, rows_local, group_size, head_dim)
    own_lse = own_lse[:, :, 0].reshape(kv_heads, rows_local, group_size)
    head_rows = jnp.arange(kv_heads, dtype=jnp.int32)[:, None]
    picked = (
        jnp.einsum(
            "htcr,thcx->hrx",
            one_hot,
            answers,
            preferred_element_type=jnp.float32,
        )
        .reshape(kv_heads, rows_local, top_count, group_size, head_dim)
    )
    picked_parts = jnp.einsum(
        "htcr,thcx->hrx", one_hot, lse_parts, preferred_element_type=jnp.float32
    )
    picked_lse = (picked_parts[..., :group_size] + picked_parts[..., group_size:]).reshape(
        kv_heads, rows_local, top_count, group_size
    )
    ceiling = jnp.maximum(own_lse, jnp.max(picked_lse, axis=2))
    own_weight = jnp.exp(own_lse - ceiling)
    far_weight = jnp.exp(picked_lse - ceiling[:, :, None])
    denominator = own_weight + jnp.sum(far_weight, axis=2)
    combined = (
        own_weight[..., None] * own_out + jnp.sum(far_weight[..., None] * picked, axis=2)
    ) / denominator[..., None]
    heads_out = (
        jnp.transpose(combined, (1, 0, 2, 3))
        .astype(jnp.bfloat16)
        .reshape(rows_local, query_heads * head_dim)
    )
    return lax.all_to_all(heads_out, "kvh", split_axis=0, concat_axis=1, tiled=True)


def solution(mesh):
    placed = (
        P("seq", "kvh", None),
        P(None, "seq", "kvh", None),
        P(None, "seq", None, "kvh", None),
        P("kvh", "seq", None),
        P(),
    )
    return jax.shard_map(
        per_device, mesh=mesh, in_specs=placed, out_specs=P(("seq", "kvh"), None), check_vma=False
    )
```

```python
import functools
import math

import jax
import jax.numpy as jnp
from jax import lax
from jax.experimental import pallas as pl
from jax.sharding import PartitionSpec as P

BLOCK_TOKENS = 2048
BLOCK_PICK_LIMIT = 2
WINDOW_SHIFTS = (8, 4, 16, 2, 1)
LOG2_E = 1.4426950408889634


def shifted(value, axis, steps):
    count = lax.axis_size(axis)
    initial, last = (max(0, -steps), min(count, count - steps))
    return lax.ppermute(value, axis, [(source, source + steps) for source in range(initial, last)])


def gather_window(stretch_kv, span_devices, companions):
    stack = stretch_kv[None]
    offsets = [0]
    results = []
    for index, step in enumerate(WINDOW_SHIFTS):
        if len(offsets) >= span_devices:
            break
        arrived = shifted(stack, "seq", step)
        if index < len(companions) and companions[index] is not None:
            arrived, done = lax.optimization_barrier((arrived, companions[index]()))
            results.append(done)
        stack = jnp.concatenate([stack, arrived], axis=0)
        offsets = offsets + [o + step for o in offsets]
    return stack, offsets, results


def attend_kernel(masked, scaling, group_size, *refs):
    if masked:
        thr_ref, q_ref, k_ref, v_ref, o_ref, lse_ref = refs
    else:
        q_ref, k_ref, v_ref, o_ref, lse_ref = refs
    q = q_ref[...]
    q = q.reshape(-1, q.shape[-1])
    scores = lax.dot_general(
        q, k_ref[...], (((1,), (1,)), ((), ())), preferred_element_type=jnp.float32
    )
    if masked:
        token = lax.broadcasted_iota(jnp.int32, (scores.shape[0], 1), 0) // group_size
        scores = jnp.where(token >= thr_ref[...], scores, -jnp.inf)
    highest = jnp.max(scores, axis=1, keepdims=True)
    raw_weights = jnp.exp2((scores - highest) * (scaling * LOG2_E))
    weight_sum = jnp.sum(raw_weights, axis=1, keepdims=True)
    blended = (
        jnp.dot(raw_weights.astype(jnp.bfloat16), v_ref[...], preferred_element_type=jnp.float32)
        / weight_sum
    )
    o_ref[...] = blended.astype(o_ref.dtype).reshape(o_ref.shape)
    log_sum = highest * scaling + jnp.log(weight_sum)
    lse_ref[...] = jnp.transpose(jnp.broadcast_to(log_sum, (log_sum.shape[0], 128)))[:8]


def attend(q, q_block, q_map, heads, tiles, keys, values, out_dtype, scaling, group_size, thr=None, out_rows=None, out_map=None):
    rows = q_block[0] * q_block[-2] if len(q_block) == 4 else q_block[-2]
    total_rows = rows * tiles
    key_count, head_dim = keys.shape[1], keys.shape[2]
    kv_spec = pl.BlockSpec((None, key_count, head_dim), lambda h, i: (h, 0, 0))
    in_specs = [pl.BlockSpec(q_block, q_map), kv_spec, kv_spec]
    operands = [q, keys, values]
    if thr is not None:
        in_specs = [pl.BlockSpec((1, key_count), lambda h, i: (0, 0))] + in_specs
        operands = [thr] + operands
    cost = pl.CostEstimate(
        flops=4 * heads * total_rows * key_count * head_dim,
        transcendentals=heads * total_rows * key_count,
        bytes_accessed=2 * (2 * heads * total_rows * head_dim + 2 * heads * key_count * head_dim),
    )
    return pl.pallas_call(
        functools.partial(attend_kernel, thr is not None, scaling, group_size),
        grid=(heads, tiles),
        in_specs=in_specs,
        out_specs=[
            pl.BlockSpec(q_block, out_map or q_map),
            pl.BlockSpec((None, None, 8, rows), lambda h, i: (h, i, 0, 0)),
        ],
        out_shape=[
            jax.ShapeDtypeStruct(((out_rows or q.shape[0]),) + q.shape[1:], out_dtype),
            jax.ShapeDtypeStruct((heads, tiles, 8, rows), jnp.float32),
        ],
        cost_estimate=cost,
    )(*operands)


def per_device(queries, stretch_kv, cache_kv, selection, block_owner):
    rows_local, query_heads, head_dim = queries.shape
    kv_heads = stretch_kv.shape[2]
    group_size = query_heads // kv_heads
    top_count = selection.shape[2]
    scaling = 1.0 / math.sqrt(head_dim)
    seq_count = lax.axis_size("seq")
    capacity = BLOCK_PICK_LIMIT
    span_devices = min(BLOCK_TOKENS // rows_local, seq_count)
    seq_place = lax.axis_index("seq")
    grouped = queries.reshape(rows_local, kv_heads, group_size, head_dim)
    requests = rows_local * top_count
    owners = jnp.arange(block_owner.shape[0], dtype=jnp.int32)
    targets = jnp.sum(
        jnp.where(selection[..., None] == owners, block_owner, 0), axis=-1
    ).reshape(kv_heads, requests)
    matches = (targets[:, :, None] == jnp.arange(seq_count, dtype=jnp.int32)[None, None, :]).astype(
        jnp.int32
    )
    places = jnp.sum((jnp.cumsum(matches, axis=1) - 1) * matches, axis=2)
    slots = targets * capacity + places
    one_hot = (
        (slots[:, None, :] == jnp.arange(seq_count * capacity, dtype=jnp.int32)[None, :, None])
        .astype(jnp.bfloat16)
        .reshape(kv_heads, seq_count, capacity, requests)
    )
    requested = jnp.repeat(jnp.swapaxes(grouped, 0, 1), top_count, axis=1)
    outgoing = jnp.einsum(
        "htcr,hrgd->thcgd", one_hot, requested, preferred_element_type=jnp.float32
    ).astype(jnp.bfloat16)
    slab = capacity * group_size
    outgoing = outgoing.reshape(seq_count, kv_heads, slab, head_dim)
    arrived = lax.all_to_all(outgoing, "seq", split_axis=0, concat_axis=0, tiled=True)
    arrived, window_start = lax.optimization_barrier((arrived, stretch_kv))
    cache_keys = jnp.swapaxes(cache_kv[0, 0], 0, 1)
    cache_values = jnp.swapaxes(cache_kv[1, 0], 0, 1)
    sources_per_tile = 32
    pieces = seq_count // sources_per_tile

    def serve_piece(piece):
        return attend(
            arrived[piece * sources_per_tile : (piece + 1) * sources_per_tile],
            (sources_per_tile, None, slab, head_dim),
            lambda h, i: (0, h, 0, 0),
            kv_heads,
            1,
            cache_keys,
            cache_values,
            jnp.bfloat16,
            scaling,
            group_size,
        )

    window, offsets, served_pieces = gather_window(
        window_start,
        span_devices,
        [None] + [functools.partial(serve_piece, piece) for piece in range(pieces)],
    )
    blocks = window.shape[0]
    served = jnp.concatenate([piece[0] for piece in served_pieces], axis=0)
    served_lse = jnp.concatenate([piece[1] for piece in served_pieces], axis=1)[:, :, 0]
    served_lse = served_lse.reshape(kv_heads, seq_count, slab)
    served_lse = jnp.swapaxes(served_lse, 0, 1)
    served, served_lse, window = lax.optimization_barrier((served, served_lse, window))
    lse_rounded = lax.reduce_precision(served_lse, exponent_bits=8, mantissa_bits=7)
    lse_high = lse_rounded.astype(jnp.bfloat16)
    lse_low = (served_lse - lse_rounded).astype(jnp.bfloat16)
    payload_width = slab * head_dim
    lse_width = 2 * slab
    lse_lanes = -(-lse_width // 128) * 128 // 2
    lse_pack = jnp.concatenate([lse_high, lse_low], axis=2)
    payload = jnp.concatenate(
        [
            served.reshape(seq_count, kv_heads, payload_width),
            jnp.pad(lse_pack, ((0, 0), (0, 0), (0, lse_lanes - lse_width))),
        ],
        axis=2,
    )
    returned = lax.all_to_all(payload, "seq", split_axis=0, concat_axis=0, tiled=True)
    answers = returned[:, :, :payload_width].reshape(seq_count, kv_heads, capacity, group_size * head_dim)
    lse_parts = returned[:, :, payload_width : payload_width + lse_width].reshape(
        seq_count, kv_heads, 2, capacity, group_size
    )
    lse_parts = jnp.swapaxes(lse_parts, 2, 3).reshape(seq_count, kv_heads, capacity, 2 * group_size)
    window_keys = jnp.transpose(window[:, 0], (2, 0, 1, 3)).reshape(kv_heads, blocks * rows_local, head_dim)
    window_values = jnp.transpose(window[:, 1], (2, 0, 1, 3)).reshape(kv_heads, blocks * rows_local, head_dim)
    key_index = jnp.arange(blocks * rows_local, dtype=jnp.int32)
    key_offset = jnp.asarray(offsets, jnp.int32)[key_index // rows_local]
    threshold = jnp.where(
        seq_place - key_offset >= 0,
        jnp.where(key_offset == 0, key_index % rows_local, 0),
        rows_local,
    )[None, :]
    window_queries = jnp.swapaxes(grouped, 0, 1).reshape(kv_heads, rows_local * group_size, head_dim)
    own_out, own_lse = attend(
        window_queries,
        (None, rows_local * group_size, head_dim),
        lambda h, i: (h, 0, 0),
        kv_heads,
        1,
        window_keys,
        window_values,
        jnp.float32,
        scaling,
        group_size,
        threshold,
    )
    own_out = own_out.reshape(kv_heads, rows_local, group_size, head_dim)
    own_lse = own_lse[:, :, 0].reshape(kv_heads, rows_local, group_size)
    head_rows = jnp.arange(kv_heads, dtype=jnp.int32)[:, None]
    picked = (
        jnp.einsum(
            "htcr,thcx->hrx",
            one_hot,
            answers,
            preferred_element_type=jnp.float32,
        )
        .reshape(kv_heads, rows_local, top_count, group_size, head_dim)
    )
    picked_parts = jnp.einsum(
        "htcr,thcx->hrx", one_hot, lse_parts, preferred_element_type=jnp.float32
    )
    picked_lse = (picked_parts[..., :group_size] + picked_parts[..., group_size:]).reshape(
        kv_heads, rows_local, top_count, group_size
    )
    ceiling = jnp.maximum(own_lse, jnp.max(picked_lse, axis=2))
    own_weight = jnp.exp(own_lse - ceiling)
    far_weight = jnp.exp(picked_lse - ceiling[:, :, None])
    denominator = own_weight + jnp.sum(far_weight, axis=2)
    combined = (
        own_weight[..., None] * own_out + jnp.sum(far_weight[..., None] * picked, axis=2)
    ) / denominator[..., None]
    heads_out = (
        jnp.transpose(combined, (1, 0, 2, 3))
        .astype(jnp.bfloat16)
        .reshape(rows_local, query_heads * head_dim)
    )
    return lax.all_to_all(heads_out, "kvh", split_axis=0, concat_axis=1, tiled=True)


def solution(mesh):
    placed = (
        P("seq", "kvh", None),
        P(None, "seq", "kvh", None),
        P(None, "seq", None, "kvh", None),
        P("kvh", "seq", None),
        P(),
    )
    return jax.shard_map(
        per_device, mesh=mesh, in_specs=placed, out_specs=P(("seq", "kvh"), None), check_vma=False
    )
```

```python
import functools
import math

import jax
import jax.numpy as jnp
from jax import lax
from jax.experimental import pallas as pl
from jax.sharding import PartitionSpec as P

BLOCK_TOKENS = 2048
BLOCK_PICK_LIMIT = 2
WINDOW_SHIFTS = (8, 4, 16, 2, 1)
LOG2_E = 1.4426950408889634


def shifted(value, axis, steps):
    count = lax.axis_size(axis)
    initial, last = (max(0, -steps), min(count, count - steps))
    return lax.ppermute(value, axis, [(source, source + steps) for source in range(initial, last)])


def gather_window(stretch_kv, span_devices, companions):
    stack = stretch_kv[None]
    offsets = [0]
    results = []
    for index, step in enumerate(WINDOW_SHIFTS):
        if len(offsets) >= span_devices:
            break
        arrived = shifted(stack, "seq", step)
        if index < len(companions) and companions[index] is not None:
            arrived, done = lax.optimization_barrier((arrived, companions[index]()))
            results.append(done)
        stack = jnp.concatenate([stack, arrived], axis=0)
        offsets = offsets + [o + step for o in offsets]
    return stack, offsets, results


def attend_kernel(masked, scaling, group_size, *refs):
    if masked:
        thr_ref, q_ref, k_ref, v_ref, o_ref, lse_ref = refs
    else:
        q_ref, k_ref, v_ref, o_ref, lse_ref = refs
    q = q_ref[...]
    q = q.reshape(-1, q.shape[-1])
    scores = lax.dot_general(
        q, k_ref[...], (((1,), (1,)), ((), ())), preferred_element_type=jnp.float32
    )
    if masked:
        token = lax.broadcasted_iota(jnp.int32, (scores.shape[0], 1), 0) // group_size
        scores = jnp.where(token >= thr_ref[...], scores, -jnp.inf)
    highest = jnp.max(scores, axis=1, keepdims=True)
    raw_weights = jnp.exp2((scores - highest) * (scaling * LOG2_E))
    weight_sum = jnp.sum(raw_weights, axis=1, keepdims=True)
    blended = (
        jnp.dot(raw_weights.astype(jnp.bfloat16), v_ref[...], preferred_element_type=jnp.float32)
        / weight_sum
    )
    o_ref[...] = blended.astype(o_ref.dtype).reshape(o_ref.shape)
    log_sum = highest * scaling + jnp.log(weight_sum)
    lse_ref[...] = jnp.transpose(jnp.broadcast_to(log_sum, (log_sum.shape[0], 128)))[:8]


def attend(q, q_block, q_map, heads, tiles, keys, values, out_dtype, scaling, group_size, thr=None, out_rows=None, out_map=None):
    rows = q_block[0] * q_block[-2] if len(q_block) == 4 else q_block[-2]
    total_rows = rows * tiles
    key_count, head_dim = keys.shape[1], keys.shape[2]
    kv_spec = pl.BlockSpec((None, key_count, head_dim), lambda h, i: (h, 0, 0))
    in_specs = [pl.BlockSpec(q_block, q_map), kv_spec, kv_spec]
    operands = [q, keys, values]
    if thr is not None:
        in_specs = [pl.BlockSpec((1, key_count), lambda h, i: (0, 0))] + in_specs
        operands = [thr] + operands
    cost = pl.CostEstimate(
        flops=4 * heads * total_rows * key_count * head_dim,
        transcendentals=heads * total_rows * key_count,
        bytes_accessed=2 * (2 * heads * total_rows * head_dim + 2 * heads * key_count * head_dim),
    )
    return pl.pallas_call(
        functools.partial(attend_kernel, thr is not None, scaling, group_size),
        grid=(heads, tiles),
        in_specs=in_specs,
        out_specs=[
            pl.BlockSpec(q_block, out_map or q_map),
            pl.BlockSpec((None, None, 8, rows), lambda h, i: (h, i, 0, 0)),
        ],
        out_shape=[
            jax.ShapeDtypeStruct(((out_rows or q.shape[0]),) + q.shape[1:], out_dtype),
            jax.ShapeDtypeStruct((heads, tiles, 8, rows), jnp.float32),
        ],
        cost_estimate=cost,
    )(*operands)


def per_device(queries, stretch_kv, cache_kv, selection, block_owner):
    rows_local, query_heads, head_dim = queries.shape
    kv_heads = stretch_kv.shape[2]
    group_size = query_heads // kv_heads
    top_count = selection.shape[2]
    scaling = 1.0 / math.sqrt(head_dim)
    seq_count = lax.axis_size("seq")
    capacity = BLOCK_PICK_LIMIT
    span_devices = min(BLOCK_TOKENS // rows_local, seq_count)
    seq_place = lax.axis_index("seq")
    grouped = queries.reshape(rows_local, kv_heads, group_size, head_dim)
    requests = rows_local * top_count
    owners = jnp.arange(block_owner.shape[0], dtype=jnp.int32)
    targets = jnp.sum(
        jnp.where(selection[..., None] == owners, block_owner, 0), axis=-1
    ).reshape(kv_heads, requests)
    matches = (targets[:, :, None] == jnp.arange(seq_count, dtype=jnp.int32)[None, None, :]).astype(
        jnp.int32
    )
    places = jnp.sum((jnp.cumsum(matches, axis=1) - 1) * matches, axis=2)
    slots = targets * capacity + places
    one_hot = (
        (slots[:, None, :] == jnp.arange(seq_count * capacity, dtype=jnp.int32)[None, :, None])
        .astype(jnp.bfloat16)
        .reshape(kv_heads, seq_count, capacity, requests)
    )
    requested = jnp.repeat(jnp.swapaxes(grouped, 0, 1), top_count, axis=1)
    outgoing = jnp.einsum(
        "htcr,hrgd->thcgd", one_hot, requested, preferred_element_type=jnp.float32
    ).astype(jnp.bfloat16)
    slab = capacity * group_size
    outgoing = outgoing.reshape(seq_count, kv_heads, slab, head_dim)
    arrived = lax.all_to_all(outgoing, "seq", split_axis=0, concat_axis=0, tiled=True)
    arrived, window_start = lax.optimization_barrier((arrived, stretch_kv))
    cache_keys = jnp.swapaxes(cache_kv[0, 0], 0, 1)
    cache_values = jnp.swapaxes(cache_kv[1, 0], 0, 1)
    sources_per_tile = 32
    pieces = seq_count // sources_per_tile

    def serve_piece(piece):
        return attend(
            arrived[piece * sources_per_tile : (piece + 1) * sources_per_tile],
            (sources_per_tile, None, slab, head_dim),
            lambda h, i: (0, h, 0, 0),
            kv_heads,
            1,
            cache_keys,
            cache_values,
            jnp.bfloat16,
            scaling,
            group_size,
        )

    window, offsets, served_pieces = gather_window(
        window_start,
        span_devices,
        [None] + [functools.partial(serve_piece, piece) for piece in range(pieces)],
    )
    blocks = window.shape[0]
    served = jnp.concatenate([piece[0] for piece in served_pieces], axis=0)
    served_lse = jnp.concatenate([piece[1] for piece in served_pieces], axis=1)[:, :, 0]
    served_lse = served_lse.reshape(kv_heads, seq_count, slab)
    served_lse = jnp.swapaxes(served_lse, 0, 1)
    served, served_lse, window = lax.optimization_barrier((served, served_lse, window))
    lse_rounded = lax.reduce_precision(served_lse, exponent_bits=8, mantissa_bits=7)
    lse_rest = served_lse - lse_rounded
    lse_middle = lax.reduce_precision(lse_rest, exponent_bits=8, mantissa_bits=7)
    lse_parts_out = [
        lse_rounded.astype(jnp.bfloat16),
        lse_middle.astype(jnp.bfloat16),
        (lse_rest - lse_middle).astype(jnp.bfloat16),
    ]
    payload_width = slab * head_dim
    lse_width = len(lse_parts_out) * slab
    lse_lanes = -(-(2 * slab) // 128) * 128 // 2
    lse_pack = jnp.concatenate(lse_parts_out, axis=2)
    payload = jnp.concatenate(
        [
            served.reshape(seq_count, kv_heads, payload_width),
            jnp.pad(lse_pack, ((0, 0), (0, 0), (0, lse_lanes - lse_width))),
        ],
        axis=2,
    )
    returned = lax.all_to_all(payload, "seq", split_axis=0, concat_axis=0, tiled=True)
    answers = returned[:, :, :payload_width].reshape(seq_count, kv_heads, capacity, group_size * head_dim)
    part_count = len(lse_parts_out)
    lse_parts = returned[:, :, payload_width : payload_width + lse_width].reshape(
        seq_count, kv_heads, part_count, capacity, group_size
    )
    lse_parts = jnp.swapaxes(lse_parts, 2, 3).reshape(
        seq_count, kv_heads, capacity, part_count * group_size
    )
    window_keys = jnp.transpose(window[:, 0], (2, 0, 1, 3)).reshape(kv_heads, blocks * rows_local, head_dim)
    window_values = jnp.transpose(window[:, 1], (2, 0, 1, 3)).reshape(kv_heads, blocks * rows_local, head_dim)
    key_index = jnp.arange(blocks * rows_local, dtype=jnp.int32)
    key_offset = jnp.asarray(offsets, jnp.int32)[key_index // rows_local]
    threshold = jnp.where(
        seq_place - key_offset >= 0,
        jnp.where(key_offset == 0, key_index % rows_local, 0),
        rows_local,
    )[None, :]
    window_queries = jnp.swapaxes(grouped, 0, 1).reshape(kv_heads, rows_local * group_size, head_dim)
    own_out, own_lse = attend(
        window_queries,
        (None, rows_local * group_size, head_dim),
        lambda h, i: (h, 0, 0),
        kv_heads,
        1,
        window_keys,
        window_values,
        jnp.float32,
        scaling,
        group_size,
        threshold,
    )
    own_out = own_out.reshape(kv_heads, rows_local, group_size, head_dim)
    own_lse = own_lse[:, :, 0].reshape(kv_heads, rows_local, group_size)
    head_rows = jnp.arange(kv_heads, dtype=jnp.int32)[:, None]
    picked = (
        jnp.einsum(
            "htcr,thcx->hrx",
            one_hot,
            answers,
            preferred_element_type=jnp.float32,
        )
        .reshape(kv_heads, rows_local, top_count, group_size, head_dim)
    )
    picked_parts = jnp.einsum(
        "htcr,thcx->hrx", one_hot, lse_parts, preferred_element_type=jnp.float32
    )
    picked_lse = (
        picked_parts[..., :group_size]
        + picked_parts[..., group_size : 2 * group_size]
        + picked_parts[..., 2 * group_size :]
    ).reshape(kv_heads, rows_local, top_count, group_size)
    ceiling = jnp.maximum(own_lse, jnp.max(picked_lse, axis=2))
    own_weight = jnp.exp(own_lse - ceiling)
    far_weight = jnp.exp(picked_lse - ceiling[:, :, None])
    denominator = own_weight + jnp.sum(far_weight, axis=2)
    combined = (
        own_weight[..., None] * own_out + jnp.sum(far_weight[..., None] * picked, axis=2)
    ) / denominator[..., None]
    heads_out = (
        jnp.transpose(combined, (1, 0, 2, 3))
        .astype(jnp.bfloat16)
        .reshape(rows_local, query_heads * head_dim)
    )
    return lax.all_to_all(heads_out, "kvh", split_axis=0, concat_axis=1, tiled=True)


def solution(mesh):
    placed = (
        P("seq", "kvh", None),
        P(None, "seq", "kvh", None),
        P(None, "seq", None, "kvh", None),
        P("kvh", "seq", None),
        P(),
    )
    return jax.shard_map(
        per_device, mesh=mesh, in_specs=placed, out_specs=P(("seq", "kvh"), None), check_vma=False
    )
```

```python
import functools
import math

import jax
import jax.numpy as jnp
from jax import lax
from jax.experimental import pallas as pl
from jax.sharding import PartitionSpec as P

BLOCK_TOKENS = 2048
BLOCK_PICK_LIMIT = 2
WINDOW_SHIFTS = (8, 4, 16, 2, 1)
LOG2_E = 1.4426950408889634


def shifted(value, axis, steps):
    count = lax.axis_size(axis)
    initial, last = (max(0, -steps), min(count, count - steps))
    return lax.ppermute(value, axis, [(source, source + steps) for source in range(initial, last)])


def gather_window(stretch_kv, span_devices, companions):
    stack = stretch_kv[None]
    offsets = [0]
    results = []
    for index, step in enumerate(WINDOW_SHIFTS):
        if len(offsets) >= span_devices:
            break
        arrived = shifted(stack, "seq", step)
        if index < len(companions) and companions[index] is not None:
            arrived, done = lax.optimization_barrier((arrived, companions[index]()))
            results.append(done)
        stack = jnp.concatenate([stack, arrived], axis=0)
        offsets = offsets + [o + step for o in offsets]
    return stack, offsets, results


def attend_kernel(masked, scaling, group_size, *refs):
    if masked:
        thr_ref, q_ref, k_ref, v_ref, o_ref, lse_ref = refs
    else:
        q_ref, k_ref, v_ref, o_ref, lse_ref = refs
    q = q_ref[...]
    q = q.reshape(-1, q.shape[-1])
    scores = lax.dot_general(
        q, k_ref[...], (((1,), (1,)), ((), ())), preferred_element_type=jnp.float32
    )
    if masked:
        token = lax.broadcasted_iota(jnp.int32, (scores.shape[0], 1), 0) // group_size
        scores = jnp.where(token >= thr_ref[...], scores, -jnp.inf)
    highest = jnp.max(scores, axis=1, keepdims=True)
    raw_weights = jnp.exp2((scores - highest) * (scaling * LOG2_E))
    weight_sum = jnp.sum(raw_weights, axis=1, keepdims=True)
    blended = (
        jnp.dot(raw_weights.astype(jnp.bfloat16), v_ref[...], preferred_element_type=jnp.float32)
        / weight_sum
    )
    o_ref[...] = blended.astype(o_ref.dtype).reshape(o_ref.shape)
    log_sum = highest * scaling + jnp.log(weight_sum)
    lse_ref[...] = jnp.transpose(jnp.broadcast_to(log_sum, (log_sum.shape[0], 128)))[:8]


def attend(q, q_block, q_map, heads, tiles, keys, values, out_dtype, scaling, group_size, thr=None, out_rows=None, out_map=None):
    rows = q_block[0] * q_block[-2] if len(q_block) == 4 else q_block[-2]
    total_rows = rows * tiles
    key_count, head_dim = keys.shape[1], keys.shape[2]
    kv_spec = pl.BlockSpec((None, key_count, head_dim), lambda h, i: (h, 0, 0))
    in_specs = [pl.BlockSpec(q_block, q_map), kv_spec, kv_spec]
    operands = [q, keys, values]
    if thr is not None:
        in_specs = [pl.BlockSpec((1, key_count), lambda h, i: (0, 0))] + in_specs
        operands = [thr] + operands
    cost = pl.CostEstimate(
        flops=4 * heads * total_rows * key_count * head_dim,
        transcendentals=heads * total_rows * key_count,
        bytes_accessed=2 * (2 * heads * total_rows * head_dim + 2 * heads * key_count * head_dim),
    )
    return pl.pallas_call(
        functools.partial(attend_kernel, thr is not None, scaling, group_size),
        grid=(heads, tiles),
        in_specs=in_specs,
        out_specs=[
            pl.BlockSpec(q_block, out_map or q_map),
            pl.BlockSpec((None, None, 8, rows), lambda h, i: (h, i, 0, 0)),
        ],
        out_shape=[
            jax.ShapeDtypeStruct(((out_rows or q.shape[0]),) + q.shape[1:], out_dtype),
            jax.ShapeDtypeStruct((heads, tiles, 8, rows), jnp.float32),
        ],
        cost_estimate=cost,
    )(*operands)


def per_device(queries, stretch_kv, cache_kv, selection, block_owner):
    rows_local, query_heads, head_dim = queries.shape
    kv_heads = stretch_kv.shape[2]
    group_size = query_heads // kv_heads
    top_count = selection.shape[2]
    scaling = 1.0 / math.sqrt(head_dim)
    seq_count = lax.axis_size("seq")
    capacity = BLOCK_PICK_LIMIT
    span_devices = min(BLOCK_TOKENS // rows_local, seq_count)
    seq_place = lax.axis_index("seq")
    grouped = queries.reshape(rows_local, kv_heads, group_size, head_dim)
    requests = rows_local * top_count
    owners = jnp.arange(block_owner.shape[0], dtype=jnp.int32)
    targets = jnp.sum(
        jnp.where(selection[..., None] == owners, block_owner, 0), axis=-1
    ).reshape(kv_heads, requests)
    matches = (targets[:, :, None] == jnp.arange(seq_count, dtype=jnp.int32)[None, None, :]).astype(
        jnp.int32
    )
    places = jnp.sum((jnp.cumsum(matches, axis=1) - 1) * matches, axis=2)
    slots = targets * capacity + places
    one_hot = (
        (slots[:, None, :] == jnp.arange(seq_count * capacity, dtype=jnp.int32)[None, :, None])
        .astype(jnp.bfloat16)
        .reshape(kv_heads, seq_count, capacity, requests)
    )
    requested = jnp.repeat(jnp.swapaxes(grouped, 0, 1), top_count, axis=1).reshape(
        kv_heads * requests, group_size, head_dim
    )
    head_ids = jnp.arange(kv_heads, dtype=jnp.int32)[:, None]
    row_of = ((targets * kv_heads + head_ids) * capacity + places).reshape(kv_heads * requests)
    spread = (
        jnp.arange(seq_count * kv_heads * capacity, dtype=jnp.int32)[:, None] == row_of[None, :]
    ).astype(jnp.bfloat16)
    outgoing = jnp.einsum(
        "Rk,kgd->Rgd", spread, requested, preferred_element_type=jnp.float32
    ).astype(jnp.bfloat16)
    slab = capacity * group_size
    outgoing = outgoing.reshape(seq_count, kv_heads, slab, head_dim)
    arrived = lax.all_to_all(outgoing, "seq", split_axis=0, concat_axis=0, tiled=True)
    arrived, window_start = lax.optimization_barrier((arrived, stretch_kv))
    cache_keys = jnp.swapaxes(cache_kv[0, 0], 0, 1)
    cache_values = jnp.swapaxes(cache_kv[1, 0], 0, 1)
    sources_per_tile = 32
    pieces = seq_count // sources_per_tile

    def serve_piece(piece):
        return attend(
            arrived[piece * sources_per_tile : (piece + 1) * sources_per_tile],
            (sources_per_tile, None, slab, head_dim),
            lambda h, i: (0, h, 0, 0),
            kv_heads,
            1,
            cache_keys,
            cache_values,
            jnp.bfloat16,
            scaling,
            group_size,
        )

    window, offsets, served_pieces = gather_window(
        window_start,
        span_devices,
        [None] + [functools.partial(serve_piece, piece) for piece in range(pieces)],
    )
    blocks = window.shape[0]
    served = jnp.concatenate([piece[0] for piece in served_pieces], axis=0)
    served_lse = jnp.concatenate([piece[1] for piece in served_pieces], axis=1)[:, :, 0]
    served_lse = served_lse.reshape(kv_heads, seq_count, slab)
    served_lse = jnp.swapaxes(served_lse, 0, 1)
    served, served_lse, window = lax.optimization_barrier((served, served_lse, window))
    lse_rounded = lax.reduce_precision(served_lse, exponent_bits=8, mantissa_bits=7)
    lse_rest = served_lse - lse_rounded
    lse_middle = lax.reduce_precision(lse_rest, exponent_bits=8, mantissa_bits=7)
    lse_parts_out = [
        lse_rounded.astype(jnp.bfloat16),
        lse_middle.astype(jnp.bfloat16),
        (lse_rest - lse_middle).astype(jnp.bfloat16),
    ]
    payload_width = slab * head_dim
    lse_width = len(lse_parts_out) * slab
    lse_lanes = -(-(2 * slab) // 128) * 128 // 2
    lse_pack = jnp.concatenate(lse_parts_out, axis=2)
    payload = jnp.concatenate(
        [
            served.reshape(seq_count, kv_heads, payload_width),
            jnp.pad(lse_pack, ((0, 0), (0, 0), (0, lse_lanes - lse_width))),
        ],
        axis=2,
    )
    returned = lax.all_to_all(payload, "seq", split_axis=0, concat_axis=0, tiled=True)
    answers = returned[:, :, :payload_width].reshape(seq_count, kv_heads, capacity, group_size * head_dim)
    part_count = len(lse_parts_out)
    lse_parts = returned[:, :, payload_width : payload_width + lse_width].reshape(
        seq_count, kv_heads, part_count, capacity, group_size
    )
    lse_parts = jnp.swapaxes(lse_parts, 2, 3).reshape(
        seq_count, kv_heads, capacity, part_count * group_size
    )
    window_keys = jnp.transpose(window[:, 0], (2, 0, 1, 3)).reshape(kv_heads, blocks * rows_local, head_dim)
    window_values = jnp.transpose(window[:, 1], (2, 0, 1, 3)).reshape(kv_heads, blocks * rows_local, head_dim)
    key_index = jnp.arange(blocks * rows_local, dtype=jnp.int32)
    key_offset = jnp.asarray(offsets, jnp.int32)[key_index // rows_local]
    threshold = jnp.where(
        seq_place - key_offset >= 0,
        jnp.where(key_offset == 0, key_index % rows_local, 0),
        rows_local,
    )[None, :]
    window_queries = jnp.swapaxes(grouped, 0, 1).reshape(kv_heads, rows_local * group_size, head_dim)
    own_out, own_lse = attend(
        window_queries,
        (None, rows_local * group_size, head_dim),
        lambda h, i: (h, 0, 0),
        kv_heads,
        1,
        window_keys,
        window_values,
        jnp.float32,
        scaling,
        group_size,
        threshold,
    )
    own_out = own_out.reshape(kv_heads, rows_local, group_size, head_dim)
    own_lse = own_lse[:, :, 0].reshape(kv_heads, rows_local, group_size)
    head_rows = jnp.arange(kv_heads, dtype=jnp.int32)[:, None]
    picked = (
        jnp.einsum(
            "htcr,thcx->hrx",
            one_hot,
            answers,
            preferred_element_type=jnp.float32,
        )
        .reshape(kv_heads, rows_local, top_count, group_size, head_dim)
    )
    picked_parts = jnp.einsum(
        "htcr,thcx->hrx", one_hot, lse_parts, preferred_element_type=jnp.float32
    )
    picked_lse = (
        picked_parts[..., :group_size]
        + picked_parts[..., group_size : 2 * group_size]
        + picked_parts[..., 2 * group_size :]
    ).reshape(kv_heads, rows_local, top_count, group_size)
    ceiling = jnp.maximum(own_lse, jnp.max(picked_lse, axis=2))
    own_weight = jnp.exp(own_lse - ceiling)
    far_weight = jnp.exp(picked_lse - ceiling[:, :, None])
    denominator = own_weight + jnp.sum(far_weight, axis=2)
    combined = (
        own_weight[..., None] * own_out + jnp.sum(far_weight[..., None] * picked, axis=2)
    ) / denominator[..., None]
    heads_out = (
        jnp.transpose(combined, (1, 0, 2, 3))
        .astype(jnp.bfloat16)
        .reshape(rows_local, query_heads * head_dim)
    )
    return lax.all_to_all(heads_out, "kvh", split_axis=0, concat_axis=1, tiled=True)


def solution(mesh):
    placed = (
        P("seq", "kvh", None),
        P(None, "seq", "kvh", None),
        P(None, "seq", None, "kvh", None),
        P("kvh", "seq", None),
        P(),
    )
    return jax.shard_map(
        per_device, mesh=mesh, in_specs=placed, out_specs=P(("seq", "kvh"), None), check_vma=False
    )
```

```python
import functools
import math

import jax
import jax.numpy as jnp
from jax import lax
from jax.experimental import pallas as pl
from jax.sharding import PartitionSpec as P

BLOCK_TOKENS = 2048
BLOCK_PICK_LIMIT = 2
WINDOW_SHIFTS = (8, 4, 16, 2, 1)
LOG2_E = 1.4426950408889634


def shifted(value, axis, steps):
    count = lax.axis_size(axis)
    initial, last = (max(0, -steps), min(count, count - steps))
    return lax.ppermute(value, axis, [(source, source + steps) for source in range(initial, last)])


def gather_window(stretch_kv, span_devices, companions):
    stack = stretch_kv[None]
    offsets = [0]
    results = []
    for index, step in enumerate(WINDOW_SHIFTS):
        if len(offsets) >= span_devices:
            break
        arrived = shifted(stack, "seq", step)
        if index < len(companions) and companions[index] is not None:
            arrived, done = lax.optimization_barrier((arrived, companions[index]()))
            results.append(done)
        stack = jnp.concatenate([stack, arrived], axis=0)
        offsets = offsets + [o + step for o in offsets]
    return stack, offsets, results


def attend_kernel(masked, scaling, group_size, *refs):
    if masked:
        thr_ref, q_ref, k_ref, v_ref, o_ref, lse_ref = refs
    else:
        q_ref, k_ref, v_ref, o_ref, lse_ref = refs
    q = q_ref[...]
    q = q.reshape(-1, q.shape[-1])
    scores = lax.dot_general(
        q, k_ref[...], (((1,), (1,)), ((), ())), preferred_element_type=jnp.float32
    )
    if masked:
        token = lax.broadcasted_iota(jnp.int32, (scores.shape[0], 1), 0) // group_size
        scores = jnp.where(token >= thr_ref[...], scores, -jnp.inf)
    highest = jnp.max(scores, axis=1, keepdims=True)
    raw_weights = jnp.exp2((scores - highest) * (scaling * LOG2_E))
    weight_sum = jnp.sum(raw_weights, axis=1, keepdims=True)
    blended = (
        jnp.dot(raw_weights.astype(jnp.bfloat16), v_ref[...], preferred_element_type=jnp.float32)
        / weight_sum
    )
    o_ref[...] = blended.astype(o_ref.dtype).reshape(o_ref.shape)
    log_sum = highest * scaling + jnp.log(weight_sum)
    lse_ref[...] = jnp.transpose(jnp.broadcast_to(log_sum, (log_sum.shape[0], 128)))[:8]


def attend(q, q_block, q_map, heads, tiles, keys, values, out_dtype, scaling, group_size, thr=None, out_rows=None, out_map=None):
    rows = q_block[0] * q_block[-2] if len(q_block) == 4 else q_block[-2]
    total_rows = rows * tiles
    key_count, head_dim = keys.shape[1], keys.shape[2]
    kv_spec = pl.BlockSpec((None, key_count, head_dim), lambda h, i: (h, 0, 0))
    in_specs = [pl.BlockSpec(q_block, q_map), kv_spec, kv_spec]
    operands = [q, keys, values]
    if thr is not None:
        in_specs = [pl.BlockSpec((1, key_count), lambda h, i: (0, 0))] + in_specs
        operands = [thr] + operands
    cost = pl.CostEstimate(
        flops=4 * heads * total_rows * key_count * head_dim,
        transcendentals=heads * total_rows * key_count,
        bytes_accessed=2 * (2 * heads * total_rows * head_dim + 2 * heads * key_count * head_dim),
    )
    return pl.pallas_call(
        functools.partial(attend_kernel, thr is not None, scaling, group_size),
        grid=(heads, tiles),
        in_specs=in_specs,
        out_specs=[
            pl.BlockSpec(q_block, out_map or q_map),
            pl.BlockSpec((None, None, 8, rows), lambda h, i: (h, i, 0, 0)),
        ],
        out_shape=[
            jax.ShapeDtypeStruct(((out_rows or q.shape[0]),) + q.shape[1:], out_dtype),
            jax.ShapeDtypeStruct((heads, tiles, 8, rows), jnp.float32),
        ],
        cost_estimate=cost,
    )(*operands)


def per_device(queries, stretch_kv, cache_kv, selection, block_owner):
    rows_local, query_heads, head_dim = queries.shape
    kv_heads = stretch_kv.shape[2]
    group_size = query_heads // kv_heads
    top_count = selection.shape[2]
    scaling = 1.0 / math.sqrt(head_dim)
    seq_count = lax.axis_size("seq")
    capacity = BLOCK_PICK_LIMIT
    span_devices = min(BLOCK_TOKENS // rows_local, seq_count)
    seq_place = lax.axis_index("seq")
    grouped = queries.reshape(rows_local, kv_heads, group_size, head_dim)
    requests = rows_local * top_count
    owners = jnp.arange(block_owner.shape[0], dtype=jnp.int32)
    targets = jnp.sum(
        jnp.where(selection[..., None] == owners, block_owner, 0), axis=-1
    ).reshape(kv_heads, requests)
    matches = (targets[:, :, None] == jnp.arange(seq_count, dtype=jnp.int32)[None, None, :]).astype(
        jnp.int32
    )
    places = jnp.sum((jnp.cumsum(matches, axis=1) - 1) * matches, axis=2)
    slots = targets * capacity + places
    one_hot = (
        (slots[:, None, :] == jnp.arange(seq_count * capacity, dtype=jnp.int32)[None, :, None])
        .astype(jnp.bfloat16)
        .reshape(kv_heads, seq_count, capacity, requests)
    )
    requested = jnp.repeat(jnp.swapaxes(grouped, 0, 1), top_count, axis=1)
    outgoing = jnp.einsum(
        "htcr,hrgd->thcgd", one_hot, requested, preferred_element_type=jnp.float32
    ).astype(jnp.bfloat16)
    slab = capacity * group_size
    outgoing = outgoing.reshape(seq_count, kv_heads, slab, head_dim)
    arrived = lax.all_to_all(outgoing, "seq", split_axis=0, concat_axis=0, tiled=True)
    arrived, window_start = lax.optimization_barrier((arrived, stretch_kv))
    cache_keys = jnp.swapaxes(cache_kv[0, 0], 0, 1)
    cache_values = jnp.swapaxes(cache_kv[1, 0], 0, 1)
    sources_per_tile = 32
    pieces = seq_count // sources_per_tile

    def serve_piece(piece):
        return attend(
            arrived[piece * sources_per_tile : (piece + 1) * sources_per_tile],
            (sources_per_tile, None, slab, head_dim),
            lambda h, i: (0, h, 0, 0),
            kv_heads,
            1,
            cache_keys,
            cache_values,
            jnp.bfloat16,
            scaling,
            group_size,
        )

    window, offsets, served_pieces = gather_window(
        window_start,
        span_devices,
        [None] + [functools.partial(serve_piece, piece) for piece in range(pieces)],
    )
    blocks = window.shape[0]
    served = jnp.concatenate([piece[0] for piece in served_pieces], axis=0)
    served_lse = jnp.concatenate([piece[1] for piece in served_pieces], axis=1)[:, :, 0]
    served_lse = served_lse.reshape(kv_heads, seq_count, slab)
    served_lse = jnp.swapaxes(served_lse, 0, 1)
    served, served_lse = lax.optimization_barrier((served, served_lse))
    lse_rounded = lax.reduce_precision(served_lse, exponent_bits=8, mantissa_bits=7)
    lse_rest = served_lse - lse_rounded
    lse_middle = lax.reduce_precision(lse_rest, exponent_bits=8, mantissa_bits=7)
    lse_parts_out = [
        lse_rounded.astype(jnp.bfloat16),
        lse_middle.astype(jnp.bfloat16),
        (lse_rest - lse_middle).astype(jnp.bfloat16),
    ]
    payload_width = slab * head_dim
    lse_width = len(lse_parts_out) * slab
    lse_lanes = -(-(2 * slab) // 128) * 128 // 2
    lse_pack = jnp.concatenate(lse_parts_out, axis=2)
    payload = jnp.concatenate(
        [
            served.reshape(seq_count, kv_heads, payload_width),
            jnp.pad(lse_pack, ((0, 0), (0, 0), (0, lse_lanes - lse_width))),
        ],
        axis=2,
    )
    returned = lax.all_to_all(payload, "seq", split_axis=0, concat_axis=0, tiled=True)
    answers = returned[:, :, :payload_width].reshape(seq_count, kv_heads, capacity, group_size * head_dim)
    part_count = len(lse_parts_out)
    lse_parts = returned[:, :, payload_width : payload_width + lse_width].reshape(
        seq_count, kv_heads, part_count, capacity, group_size
    )
    lse_parts = jnp.swapaxes(lse_parts, 2, 3).reshape(
        seq_count, kv_heads, capacity, part_count * group_size
    )
    window_keys = jnp.transpose(window[:, 0], (2, 0, 1, 3)).reshape(kv_heads, blocks * rows_local, head_dim)
    window_values = jnp.transpose(window[:, 1], (2, 0, 1, 3)).reshape(kv_heads, blocks * rows_local, head_dim)
    key_index = jnp.arange(blocks * rows_local, dtype=jnp.int32)
    key_offset = jnp.asarray(offsets, jnp.int32)[key_index // rows_local]
    threshold = jnp.where(
        seq_place - key_offset >= 0,
        jnp.where(key_offset == 0, key_index % rows_local, 0),
        rows_local,
    )[None, :]
    window_queries = jnp.swapaxes(grouped, 0, 1).reshape(kv_heads, rows_local * group_size, head_dim)
    own_out, own_lse = attend(
        window_queries,
        (None, rows_local * group_size, head_dim),
        lambda h, i: (h, 0, 0),
        kv_heads,
        1,
        window_keys,
        window_values,
        jnp.float32,
        scaling,
        group_size,
        threshold,
    )
    own_out = own_out.reshape(kv_heads, rows_local, group_size, head_dim)
    own_lse = own_lse[:, :, 0].reshape(kv_heads, rows_local, group_size)
    head_rows = jnp.arange(kv_heads, dtype=jnp.int32)[:, None]
    picked = (
        jnp.einsum(
            "htcr,thcx->hrx",
            one_hot,
            answers,
            preferred_element_type=jnp.float32,
        )
        .reshape(kv_heads, rows_local, top_count, group_size, head_dim)
    )
    picked_parts = jnp.einsum(
        "htcr,thcx->hrx", one_hot, lse_parts, preferred_element_type=jnp.float32
    )
    picked_lse = (
        picked_parts[..., :group_size]
        + picked_parts[..., group_size : 2 * group_size]
        + picked_parts[..., 2 * group_size :]
    ).reshape(kv_heads, rows_local, top_count, group_size)
    ceiling = jnp.maximum(own_lse, jnp.max(picked_lse, axis=2))
    own_weight = jnp.exp(own_lse - ceiling)
    far_weight = jnp.exp(picked_lse - ceiling[:, :, None])
    denominator = own_weight + jnp.sum(far_weight, axis=2)
    combined = (
        own_weight[..., None] * own_out + jnp.sum(far_weight[..., None] * picked, axis=2)
    ) / denominator[..., None]
    heads_out = (
        jnp.transpose(combined, (1, 0, 2, 3))
        .astype(jnp.bfloat16)
        .reshape(rows_local, query_heads * head_dim)
    )
    return lax.all_to_all(heads_out, "kvh", split_axis=0, concat_axis=1, tiled=True)


def solution(mesh):
    placed = (
        P("seq", "kvh", None),
        P(None, "seq", "kvh", None),
        P(None, "seq", None, "kvh", None),
        P("kvh", "seq", None),
        P(),
    )
    return jax.shard_map(
        per_device, mesh=mesh, in_specs=placed, out_specs=P(("seq", "kvh"), None), check_vma=False
    )
```
